512 devices in a mesh: seq: 32 (over x, z_lo, core), tp: 16 (over y, z_hi).
Axes of the slice: x: 4, y: 8, z: 8 (z_hi: 2, z_lo: 4; z = z_hi * 4 + z_lo), core: 2. Of those that a mesh axis runs over, the one named last changes fastest.
Arguments:
- q_in: bfloat16 [16384, 4096], P('seq', 'tp'), may hold values from -40 to 40
- k_in: bfloat16 [16384, 4096], P('seq', 'tp'), may hold values from -40 to 40
- v_in: bfloat16 [16384, 4096], P('seq', 'tp'), may hold values from -6 to 6
- q_gain: float32 [4096], P('tp'), may hold values from 0.1 to 1.9
- k_gain: float32 [4096], P('tp'), may hold values from 0.1 to 1.9
- d_out: bfloat16 [16384, 4096], P('seq', 'tp'), may hold values from -6 to 6
- counts: int32 [64], replicated, may hold values from 128 to 256, as said below
- windows: int32 [32], P('tp'), may hold values from 1 to 2
Outputs:
- attn_out: bfloat16 [16384, 4096], P('seq', 'tp')
- grad_q: bfloat16 [16384, 4096], P('seq', 'tp')
- grad_k: bfloat16 [16384, 4096], P('seq', 'tp')
- grad_v: bfloat16 [16384, 4096], P('seq', 'tp')
The draws below stay inside these ranges and needn't reach their ends.
Inputs may be any that keep to these rules, and one draw needn't show every extreme that they name: `counts`: each count is a multiple of 128; slots at or beyond a frame's count are padding; some frame is full.
All inputs are finite; a program needn't handle non-finite values.
Results may differ from the reference program's by a relative error of at most 0.02.
The reference program's roundings to bfloat16 on the way (of `prob`, `grad_mask` and `dscore`) count: a program that leaves them out, or rounds other values in their place, can miss the bound.
Values may be sent and summed in bfloat16 or wider, within the bound.
No kernel may reach another device: no remote copies, remote signals or barrier semaphores. Data moves between devices by JAX's collectives and lax.ppermute only.
A program may use at most 64 MiB of HBM per device.

```python
import jax
import jax.numpy as jnp
from jax import lax

HD = 128
HEADS = 32
QUANT = 128
CAP = 256
F_DEV = 2
FRAMES = 64
TOKENS = 16384
WIDTH = 4096


def qk_fields(key):
    total_rows = FRAMES * CAP
    subkeys = jax.random.split(key, 6)
    head_of = jnp.arange(WIDTH) // HD
    rise = jnp.exp(jnp.log(3.0) * head_of.astype(jnp.float32) / max(HEADS - 1, 1))
    jitter = jnp.exp(jax.random.uniform(subkeys[0], (WIDTH,), minval=0.0, maxval=jnp.log(3.3)))
    columns = rise * jitter
    row_q = jnp.exp(jax.random.uniform(subkeys[1], (total_rows, 1), minval=0.0, maxval=jnp.log(10.0)))
    row_k = jnp.exp(jax.random.uniform(subkeys[2], (total_rows, 1), minval=0.0, maxval=jnp.log(10.0)))
    base_q = jnp.clip(jax.random.normal(subkeys[4], (total_rows, WIDTH)), -4.0, 4.0)
    base_k = jnp.clip(jax.random.normal(subkeys[5], (total_rows, WIDTH)), -4.0, 4.0)
    queries = base_q * row_q * columns / 10.0
    key_field = base_k * row_k * columns / 10.0
    return (jnp.clip(queries, -40.0, 40.0), jnp.clip(key_field, -40.0, 40.0))


def draw_q_in(key, part):
    return qk_fields(jax.random.fold_in(key, 7))[0].astype(jnp.bfloat16)


def draw_k_in(key, part):
    return qk_fields(jax.random.fold_in(key, 7))[1].astype(jnp.bfloat16)


def draw_counts(key, part):
    first, second = jax.random.split(jax.random.fold_in(key, 3))
    levels = jax.random.randint(first, (FRAMES,), 1, CAP // QUANT + 1)
    chosen = jax.random.randint(second, (), 0, FRAMES)
    levels = jnp.where(jnp.arange(FRAMES) == chosen, CAP // QUANT, levels)
    return (levels * QUANT).astype(jnp.int32)


def draw_windows(key, part):
    first, second = jax.random.split(jax.random.fold_in(key, 5))
    lengths = jax.random.randint(first, (HEADS,), 1, F_DEV + 1)
    chosen = jax.random.randint(second, (), 0, HEADS)
    lengths = jnp.where(jnp.arange(HEADS) == chosen, F_DEV, lengths)
    return lengths.astype(jnp.int32)


def level_of(key, dims, cuts, least, high):
    factor_of, own = 1.0, jax.random.fold_in(key, 6)
    for dim, parts in cuts:
        steps = jnp.exp(jax.random.uniform(jax.random.fold_in(own, dim), (parts,), jnp.float32, least / len(cuts), high / len(cuts)))
        factor_of = factor_of * jnp.repeat(steps, dims[dim] // parts).reshape([-1 if axis == dim else 1 for axis in range(len(dims))])
    return factor_of


def noise(rng, shape, width, limit, cuts=(), kind=jnp.bfloat16):
    entries = jax.random.normal(rng, shape, jnp.float32) * width
    if len(cuts) > 0:
        entries = level_of(rng, shape, cuts, -0.22, 0.18) * entries
    return jnp.clip(entries, min=-limit, max=limit).astype(kind)


def setup_inputs(seed: int = 0) -> dict:
    arg_keys = jax.random.split(jax.random.key(seed), 9)
    q_in = draw_q_in(jax.random.fold_in(arg_keys[8], 71), 0)
    k_in = draw_k_in(jax.random.fold_in(arg_keys[8], 71), 0)
    v_in = noise(arg_keys[2], (TOKENS, WIDTH), 1.0, 6.0, ((0, 32), (1, 16)))
    q_gain = jnp.clip(1.0 + 0.18 * jax.random.normal(arg_keys[3], (WIDTH,), jnp.float32), 0.1, 1.9)
    k_gain = jnp.clip(1.0 + 0.18 * jax.random.normal(arg_keys[4], (WIDTH,), jnp.float32), 0.1, 1.9)
    d_out = noise(arg_keys[5], (TOKENS, WIDTH), 1.0, 6.0, ((0, 32), (1, 16)))
    counts = draw_counts(jax.random.fold_in(arg_keys[8], 71), 0)
    windows = draw_windows(jax.random.fold_in(arg_keys[8], 71), 0)
    return {"q_in": q_in, "k_in": k_in, "v_in": v_in, "q_gain": q_gain, "k_gain": k_gain, "d_out": d_out, "counts": counts, "windows": windows}


EPS = 1e-06
NEG = -1e+30

def to_half(value):
    return lax.optimization_barrier(value.astype(jnp.bfloat16)).astype(jnp.float32)

def stack_offsets(padded, before, count):
    blocks = [padded[before - offset:before - offset + count] for offset in range(before + 1)]
    return jnp.concatenate(blocks, axis=1)

def fold_offsets(grads, before, count, slots):
    result = jnp.zeros((before + count, slots) + grads.shape[2:], jnp.float32)
    for offset in range(before + 1):
        piece = grads[:, offset * slots:(offset + 1) * slots]
        result = result + jnp.pad(piece, ((before - offset, offset), (0, 0), (0, 0)))
    return result

def attend(q_head, g_head, k_set, v_set, visible, row_live):
    factor = HD ** (-0.5)
    scores = jnp.einsum('fqd,fkd->fqk', q_head, k_set, preferred_element_type=jnp.float32) * factor
    scores = jnp.where(visible[:, None, :], scores, NEG)
    row_max = lax.optimization_barrier(jnp.max(scores, axis=2, keepdims=True))
    row_sum = lax.optimization_barrier(jnp.sum(jnp.exp(scores - row_max), axis=2, keepdims=True))
    lse = row_max + jnp.log(row_sum)
    prob_wide = jnp.exp(scores - lse)
    prob = to_half(prob_wide)
    out_wide = jnp.einsum('fqk,fkd->fqd', prob, v_set, preferred_element_type=jnp.float32)
    attn = to_half(jnp.where(row_live[:, :, None], out_wide, 0.0))
    delta = lax.optimization_barrier(jnp.sum(g_head * attn, axis=2))
    dprob = jnp.einsum('fqd,fkd->fqk', g_head, v_set, preferred_element_type=jnp.float32)
    dscore = to_half(prob_wide * (dprob - delta[:, :, None]) * factor)
    grad_qh = jnp.einsum('fqk,fkd->fqd', dscore, k_set, preferred_element_type=jnp.float32)
    grad_kh = jnp.einsum('fqk,fqd->fkd', dscore, q_head, preferred_element_type=jnp.float32)
    grad_vh = jnp.einsum('fqk,fqd->fkd', prob, g_head, preferred_element_type=jnp.float32)
    return (attn, grad_qh, grad_kh, grad_vh)

def reference(q_in, k_in, v_in, q_gain, k_gain, d_out, counts, windows):
    q_float = q_in.astype(jnp.float32)
    k_float = k_in.astype(jnp.float32)
    q_rinv = lax.rsqrt(lax.optimization_barrier(jnp.sum(q_float * q_float, axis=1, keepdims=True)) / WIDTH + EPS)
    k_rinv = lax.rsqrt(lax.optimization_barrier(jnp.sum(k_float * k_float, axis=1, keepdims=True)) / WIDTH + EPS)
    q_norm = (q_float * q_rinv * q_gain).astype(jnp.bfloat16)
    k_norm = (k_float * k_rinv * k_gain).astype(jnp.bfloat16)
    slot_index = jnp.arange(CAP, dtype=jnp.int32)
    live = slot_index[None, :] < counts[:, None]
    grad_mask = jnp.where(live.reshape(TOKENS)[:, None], d_out, jnp.zeros_like(d_out))

    def split_heads(value):
        return value.reshape(FRAMES, CAP, HEADS, HD).transpose(2, 0, 1, 3)
    frame_ids = jnp.arange(FRAMES, dtype=jnp.int32)
    offsets = jnp.arange((F_DEV + 1) * CAP, dtype=jnp.int32) // CAP
    pad_live = jnp.concatenate([jnp.zeros((F_DEV, CAP), dtype=bool), live], axis=0)
    live_stack = stack_offsets(pad_live[:, :, None], F_DEV, FRAMES)[:, :, 0]
    reach = frame_ids[:, None] - offsets[None, :] >= 0
    base_mask = live_stack & reach
    anchor_live = slot_index < counts[0]
    split = (F_DEV + 1) * CAP

    def per_head(items):
        q_head, k_head, v_head, g_head, window = items
        k_wide = k_head.astype(jnp.float32)
        v_wide = v_head.astype(jnp.float32)
        front = jnp.zeros((F_DEV, CAP, HD), jnp.float32)
        k_set = jnp.concatenate([stack_offsets(jnp.concatenate([front, k_wide], axis=0), F_DEV, FRAMES), jnp.broadcast_to(k_wide[0][None], (FRAMES, CAP, HD))], axis=1)
        v_set = jnp.concatenate([stack_offsets(jnp.concatenate([front, v_wide], axis=0), F_DEV, FRAMES), jnp.broadcast_to(v_wide[0][None], (FRAMES, CAP, HD))], axis=1)
        visible = jnp.concatenate([base_mask & (offsets[None, :] <= window), (frame_ids[:, None] - window > 0) & anchor_live[None, :]], axis=1)
        attn, grad_qh, grad_kh, grad_vh = attend(q_head.astype(jnp.float32), g_head.astype(jnp.float32), k_set, v_set, visible, live)
        grad_kf = fold_offsets(grad_kh[:, :split], F_DEV, FRAMES, CAP)[F_DEV:]
        grad_kf = grad_kf.at[0].add(lax.optimization_barrier(jnp.sum(grad_kh[:, split:], axis=0)))
        grad_vf = fold_offsets(grad_vh[:, :split], F_DEV, FRAMES, CAP)[F_DEV:]
        grad_vf = grad_vf.at[0].add(lax.optimization_barrier(jnp.sum(grad_vh[:, split:], axis=0)))
        return (attn.astype(jnp.bfloat16), grad_qh, grad_kf, grad_vf.astype(jnp.bfloat16))
    attn_h, grad_qh, grad_kh, grad_vh = lax.map(per_head, (split_heads(q_norm), split_heads(k_norm), split_heads(v_in), split_heads(grad_mask), windows))

    def merge_heads(value):
        return value.transpose(1, 2, 0, 3).reshape(TOKENS, WIDTH)
    attn_out = merge_heads(attn_h)
    grad_v = merge_heads(grad_vh)
    q_scaled = merge_heads(grad_qh) * q_gain
    k_scaled = merge_heads(grad_kh) * k_gain
    q_dot = lax.optimization_barrier(jnp.sum(q_float * q_scaled, axis=1, keepdims=True))
    k_dot = lax.optimization_barrier(jnp.sum(k_float * k_scaled, axis=1, keepdims=True))
    grad_q = (q_rinv * q_scaled - q_float * q_rinv ** 3 * q_dot / WIDTH).astype(jnp.bfloat16)
    grad_k = (k_rinv * k_scaled - k_float * k_rinv ** 3 * k_dot / WIDTH).astype(jnp.bfloat16)
    return (attn_out, grad_q, grad_k, grad_v)
```

```python
import jax
import jax.numpy as jnp
from jax import lax
from jax.sharding import PartitionSpec as P

HD = 128
CAP = 256
F_DEV = 2
WIDTH = 4096


EPS = 1e-06
NEG = -1e30


def shifted(block, axis, distance):
    devices = range(lax.axis_size(axis))
    route = [(i - distance, i) for i in devices if i - distance in devices]
    return lax.ppermute(block, axis, route)


def xor_psum(values, axis):
    n = lax.axis_size(axis)
    if n & (n - 1):
        return lax.psum(values, axis)
    step = 1
    while step < n:
        got = lax.ppermute(values, axis, [(i, i ^ step) for i in range(n)])
        values = jax.tree.map(jnp.add, values, got)
        step *= 2
    return values


def tree_plan(n):
    fans, m = [], n
    if m % 2 == 0 and (m.bit_length() - 1) % 2 == 1 and m & (m - 1) == 0:
        fans.append(2)
        m //= 2
    while m > 1:
        f = 4 if m % 4 == 0 else next(p for p in range(2, m + 1) if m % p == 0)
        fans.append(f)
        m //= f
    plan, step = [], 1
    for f in fans:
        plan.append((step, f))
        step *= f
    return plan


def tree_bcast(values, axis):
    n = lax.axis_size(axis)
    me = lax.axis_index(axis)
    for step, fan in reversed(tree_plan(n)):
        span = step * fan
        got = values
        for j in range(1, fan):
            route = [(i, i + j * step) for i in range(0, n, span) if i + j * step < n]
            arrived = lax.ppermute(values, axis, route)
            hit = me % span == j * step
            got = jax.tree.map(lambda a, g: jnp.where(hit, a, g), arrived, got)
        values = got
    return values


def tree_reduce(values, axis, wire):
    n = lax.axis_size(axis)
    for step, fan in tree_plan(n):
        span = step * fan
        total = values
        for j in range(1, fan):
            route = [(i + j * step, i) for i in range(0, n, span) if i + j * step < n]
            sent = jax.tree.map(lambda a: a.astype(wire), values)
            arrived = lax.ppermute(sent, axis, route)
            total = jax.tree.map(lambda t, a: t + a.astype(t.dtype), total, arrived)
        values = total
    return values


def stack_offsets(padded, before, count):
    blocks = [padded[before - offset : before - offset + count] for offset in range(before + 1)]
    return jnp.concatenate(blocks, axis=1)


def fold_offsets(grads, before, count, slots):
    result = jnp.zeros((before + count, slots) + grads.shape[2:], jnp.float32)
    for offset in range(before + 1):
        piece = grads[:, offset * slots : (offset + 1) * slots]
        result = result + jnp.pad(piece, ((before - offset, offset), (0, 0), (0, 0)))
    return result


def attend(q_head, g_head, k_set, v_set, visible, row_live):
    factor = HD ** (-0.5)
    scores = jnp.einsum("fqd,fkd->fqk", q_head, k_set, preferred_element_type=jnp.float32) * factor
    scores = jnp.where(visible[:, None, :], scores, NEG)
    row_max = jnp.max(scores, axis=2, keepdims=True)
    row_sum = jnp.sum(jnp.exp(scores - row_max), axis=2, keepdims=True)
    lse = row_max + jnp.log(row_sum)
    prob_wide = jnp.exp(scores - lse)
    prob = prob_wide.astype(jnp.bfloat16)
    out_wide = jnp.einsum("fqk,fkd->fqd", prob, v_set, preferred_element_type=jnp.float32)
    attn = lax.optimization_barrier(
        jnp.where(row_live[:, :, None], out_wide, 0.0).astype(jnp.bfloat16)
    )
    delta = jnp.sum(g_head.astype(jnp.float32) * attn.astype(jnp.float32), axis=2)
    dprob = jnp.einsum("fqd,fkd->fqk", g_head, v_set, preferred_element_type=jnp.float32)
    dscore = (prob_wide * (dprob - delta[:, :, None]) * factor).astype(jnp.bfloat16)
    grad_qh = jnp.einsum("fqk,fkd->fqd", dscore, k_set, preferred_element_type=jnp.float32)
    grad_kh = jnp.einsum("fqk,fqd->fkd", dscore, q_head, preferred_element_type=jnp.float32)
    grad_vh = jnp.einsum("fqk,fqd->fkd", prob, g_head, preferred_element_type=jnp.float32)
    return (attn, lse[:, :, 0], delta, grad_qh, grad_kh, grad_vh)


def on_device(q_in, k_in, v_in, q_gain, k_gain, d_out, counts, windows):
    row_count, local_width = q_in.shape
    local_heads = local_width // HD
    device = lax.axis_index("seq")
    q_float = q_in.astype(jnp.float32)
    k_float = k_in.astype(jnp.float32)
    q_power, k_power = xor_psum(
        (jnp.sum(q_float * q_float, axis=1), jnp.sum(k_float * k_float, axis=1)), "tp"
    )
    q_rinv = lax.rsqrt(q_power / WIDTH + EPS)[:, None]
    k_rinv = lax.rsqrt(k_power / WIDTH + EPS)[:, None]
    q_norm = (q_float * q_rinv * q_gain).astype(jnp.bfloat16)
    k_norm = (k_float * k_rinv * k_gain).astype(jnp.bfloat16)
    padded_counts = jnp.concatenate([jnp.zeros((F_DEV,), jnp.int32), counts])
    near_counts = lax.dynamic_slice_in_dim(padded_counts, device * F_DEV, 2 * F_DEV)
    slot_index = jnp.arange(CAP, dtype=jnp.int32)
    near_live = slot_index[None, :] < near_counts[:, None]
    row_live = near_live[F_DEV:]
    grad_mask = jnp.where(row_live.reshape(row_count)[:, None], d_out, jnp.zeros_like(d_out))
    halo_k, halo_v = shifted((k_norm, v_in), "seq", 1)
    anchor_k, anchor_v = tree_bcast((k_norm[:CAP], v_in[:CAP]), "seq")
    k_near = jnp.concatenate([halo_k, k_norm], axis=0).reshape(2 * F_DEV, CAP, local_width)
    v_near = jnp.concatenate([halo_v, v_in], axis=0).reshape(2 * F_DEV, CAP, local_width)
    k_set = jnp.concatenate(
        [
            stack_offsets(k_near, F_DEV, F_DEV),
            jnp.broadcast_to(anchor_k[None], (F_DEV, CAP, local_width)),
        ],
        axis=1,
    )
    v_set = jnp.concatenate(
        [
            stack_offsets(v_near, F_DEV, F_DEV),
            jnp.broadcast_to(anchor_v[None], (F_DEV, CAP, local_width)),
        ],
        axis=1,
    )

    def to_heads(value):
        return value.reshape(value.shape[0], value.shape[1], local_heads, HD).transpose(2, 0, 1, 3)

    def from_heads(value):
        return value.transpose(1, 2, 0, 3).reshape(value.shape[1], value.shape[2], local_heads * HD)

    frame_local = jnp.arange(F_DEV, dtype=jnp.int32)
    offsets = jnp.arange((F_DEV + 1) * CAP, dtype=jnp.int32) // CAP
    live_stack = stack_offsets(near_live[:, :, None], F_DEV, F_DEV)[:, :, 0]
    reach = device * F_DEV + frame_local[:, None] - offsets[None, :] >= 0
    within = offsets[None, None, :] <= windows[:, None, None]
    anchor_ok = device * F_DEV + frame_local[None, :] - windows[:, None] > 0
    anchor_live = slot_index < counts[0]
    visible = jnp.concatenate(
        [(live_stack & reach)[None] & within, anchor_ok[:, :, None] & anchor_live[None, None, :]],
        axis=2,
    )

    def per_head(items):
        q_head, g_head, k_head, v_head, seen = items
        return attend(q_head, g_head, k_head, v_head, seen, row_live)

    q_heads = to_heads(q_norm.reshape(F_DEV, CAP, local_width))
    g_heads = to_heads(grad_mask.reshape(F_DEV, CAP, local_width))
    attn_h, lse_h, delta_h, grad_qh, grad_kh, grad_vh = lax.map(
        per_head, (q_heads, g_heads, to_heads(k_set), to_heads(v_set), visible)
    )
    attn_out = from_heads(attn_h).reshape(row_count, local_width)
    grad_qn = from_heads(grad_qh).reshape(row_count, local_width)
    grad_k_all = from_heads(grad_kh)
    grad_v_all = from_heads(grad_vh)
    split = (F_DEV + 1) * CAP
    grad_k_near = fold_offsets(grad_k_all[:, :split], F_DEV, F_DEV, CAP)
    grad_v_near = fold_offsets(grad_v_all[:, :split], F_DEV, F_DEV, CAP)
    grad_k_anchor = jnp.sum(grad_k_all[:, split:], axis=0)
    grad_v_anchor = jnp.sum(grad_v_all[:, split:], axis=0)
    back_k, back_v = shifted((grad_k_near[:F_DEV], grad_v_near[:F_DEV]), "seq", -1)
    grad_k_own = grad_k_near[F_DEV:] + back_k
    grad_v_own = grad_v_near[F_DEV:] + back_v
    anchor_gk, anchor_gv = tree_reduce((grad_k_anchor, grad_v_anchor), "seq", jnp.bfloat16)
    first_device = device == 0
    grad_k_own = grad_k_own.at[0].add(jnp.where(first_device, anchor_gk, 0.0))
    grad_v_own = grad_v_own.at[0].add(jnp.where(first_device, anchor_gv, 0.0))
    q_scaled = grad_qn * q_gain
    k_scaled = grad_k_own.reshape(row_count, local_width) * k_gain
    q_dot = xor_psum(jnp.sum(q_float * q_scaled, axis=1), "tp")
    k_dot = xor_psum(jnp.sum(k_float * k_scaled, axis=1), "tp")
    grad_q = (q_rinv * q_scaled - q_float * q_rinv**3 * q_dot[:, None] / WIDTH).astype(jnp.bfloat16)
    grad_k = (k_rinv * k_scaled - k_float * k_rinv**3 * k_dot[:, None] / WIDTH).astype(jnp.bfloat16)
    grad_v = grad_v_own.reshape(row_count, local_width).astype(jnp.bfloat16)
    return (attn_out, grad_q, grad_k, grad_v)


def solution(mesh):
    return jax.shard_map(
        on_device,
        mesh=mesh,
        in_specs=(
            P("seq", "tp"),
            P("seq", "tp"),
            P("seq", "tp"),
            P("tp"),
            P("tp"),
            P("seq", "tp"),
            P(),
            P("tp"),
        ),
        out_specs=(P("seq", "tp"), P("seq", "tp"), P("seq", "tp"), P("seq", "tp")),
        check_vma=False,
    )
```

```python
import jax
import jax.numpy as jnp
from jax import lax
from jax.sharding import PartitionSpec as P

HD = 128
CAP = 256
F_DEV = 2
WIDTH = 4096


EPS = 1e-06
NEG = -1e30


def shifted(block, axis, distance):
    devices = range(lax.axis_size(axis))
    route = [(i - distance, i) for i in devices if i - distance in devices]
    return lax.ppermute(block, axis, route)


def xor_psum(values, axis):
    n = lax.axis_size(axis)
    if n & (n - 1):
        return lax.psum(values, axis)
    step = 1
    while step < n:
        got = lax.ppermute(values, axis, [(i, i ^ step) for i in range(n)])
        values = jax.tree.map(jnp.add, values, got)
        step *= 2
    return values


def tree_plan(n):
    fans, m = [], n
    if m % 2 == 0 and (m.bit_length() - 1) % 2 == 1 and m & (m - 1) == 0:
        fans.append(2)
        m //= 2
    while m > 1:
        f = 4 if m % 4 == 0 else next(p for p in range(2, m + 1) if m % p == 0)
        fans.append(f)
        m //= f
    plan, step = [], 1
    for f in fans:
        plan.append((step, f))
        step *= f
    return plan


def tree_bcast(values, axis):
    n = lax.axis_size(axis)
    me = lax.axis_index(axis)
    for step, fan in reversed(tree_plan(n)):
        span = step * fan
        got = values
        for j in range(1, fan):
            route = [(i, i + j * step) for i in range(0, n, span) if i + j * step < n]
            arrived = lax.ppermute(values, axis, route)
            hit = me % span == j * step
            got = jax.tree.map(lambda a, g: jnp.where(hit, a, g), arrived, got)
        values = got
    return values


def tree_reduce(values, axis, wire):
    n = lax.axis_size(axis)
    for step, fan in tree_plan(n):
        span = step * fan
        total = values
        for j in range(1, fan):
            route = [(i + j * step, i) for i in range(0, n, span) if i + j * step < n]
            sent = jax.tree.map(lambda a: a.astype(wire), values)
            arrived = lax.ppermute(sent, axis, route)
            total = jax.tree.map(lambda t, a: t + a.astype(t.dtype), total, arrived)
        values = total
    return values


def stack_offsets(padded, before, count):
    blocks = [padded[before - offset : before - offset + count] for offset in range(before + 1)]
    return jnp.concatenate(blocks, axis=1)


def fold_offsets(grads, before, count, slots):
    result = jnp.zeros((before + count, slots) + grads.shape[2:], jnp.float32)
    for offset in range(before + 1):
        piece = grads[:, offset * slots : (offset + 1) * slots]
        result = result + jnp.pad(piece, ((before - offset, offset), (0, 0), (0, 0)))
    return result


def attend(q_head, g_head, k_set, v_set, visible, row_live):
    factor = HD ** (-0.5)
    scores = jnp.einsum("fqd,fkd->fqk", q_head, k_set, preferred_element_type=jnp.float32) * factor
    scores = jnp.where(visible[:, None, :], scores, NEG)
    row_max = jnp.max(scores, axis=2, keepdims=True)
    row_sum = jnp.sum(jnp.exp(scores - row_max), axis=2, keepdims=True)
    lse = row_max + jnp.log(row_sum)
    prob_wide = jnp.exp(scores - lse)
    prob = prob_wide.astype(jnp.bfloat16)
    out_wide = jnp.einsum("fqk,fkd->fqd", prob, v_set, preferred_element_type=jnp.float32)
    attn = lax.optimization_barrier(
        jnp.where(row_live[:, :, None], out_wide, 0.0).astype(jnp.bfloat16)
    )
    delta = jnp.sum(g_head.astype(jnp.float32) * attn.astype(jnp.float32), axis=2)
    dprob = jnp.einsum("fqd,fkd->fqk", g_head, v_set, preferred_element_type=jnp.float32)
    dscore = (prob_wide * (dprob - delta[:, :, None]) * factor).astype(jnp.bfloat16)
    grad_qh = jnp.einsum("fqk,fkd->fqd", dscore, k_set, preferred_element_type=jnp.float32)
    grad_kh = jnp.einsum("fqk,fqd->fkd", dscore, q_head, preferred_element_type=jnp.float32)
    grad_vh = jnp.einsum("fqk,fqd->fkd", prob, g_head, preferred_element_type=jnp.float32)
    return (attn, lse[:, :, 0], delta, grad_qh, grad_kh, grad_vh)


def on_device(q_in, k_in, v_in, q_gain, k_gain, d_out, counts, windows):
    row_count, local_width = q_in.shape
    local_heads = local_width // HD
    device = lax.axis_index("seq")
    q_float = q_in.astype(jnp.float32)
    k_float = k_in.astype(jnp.float32)
    q_power, k_power = xor_psum(
        jnp.stack([jnp.sum(q_float * q_float, axis=1), jnp.sum(k_float * k_float, axis=1)]), "tp"
    )
    q_rinv = lax.rsqrt(q_power / WIDTH + EPS)[:, None]
    k_rinv = lax.rsqrt(k_power / WIDTH + EPS)[:, None]
    q_norm = (q_float * q_rinv * q_gain).astype(jnp.bfloat16)
    k_norm = (k_float * k_rinv * k_gain).astype(jnp.bfloat16)
    padded_counts = jnp.concatenate([jnp.zeros((F_DEV,), jnp.int32), counts])
    near_counts = lax.dynamic_slice_in_dim(padded_counts, device * F_DEV, 2 * F_DEV)
    slot_index = jnp.arange(CAP, dtype=jnp.int32)
    near_live = slot_index[None, :] < near_counts[:, None]
    row_live = near_live[F_DEV:]
    grad_mask = jnp.where(row_live.reshape(row_count)[:, None], d_out, jnp.zeros_like(d_out))
    halo_k, halo_v = shifted(jnp.stack([k_norm, v_in]), "seq", 1)
    anchor_k, anchor_v = tree_bcast(jnp.stack([k_norm[:CAP], v_in[:CAP]]), "seq")
    k_near = jnp.concatenate([halo_k, k_norm], axis=0).reshape(2 * F_DEV, CAP, local_width)
    v_near = jnp.concatenate([halo_v, v_in], axis=0).reshape(2 * F_DEV, CAP, local_width)
    k_set = jnp.concatenate(
        [
            stack_offsets(k_near, F_DEV, F_DEV),
            jnp.broadcast_to(anchor_k[None], (F_DEV, CAP, local_width)),
        ],
        axis=1,
    )
    v_set = jnp.concatenate(
        [
            stack_offsets(v_near, F_DEV, F_DEV),
            jnp.broadcast_to(anchor_v[None], (F_DEV, CAP, local_width)),
        ],
        axis=1,
    )

    def to_heads(value):
        return value.reshape(value.shape[0], value.shape[1], local_heads, HD).transpose(2, 0, 1, 3)

    def from_heads(value):
        return value.transpose(1, 2, 0, 3).reshape(value.shape[1], value.shape[2], local_heads * HD)

    frame_local = jnp.arange(F_DEV, dtype=jnp.int32)
    offsets = jnp.arange((F_DEV + 1) * CAP, dtype=jnp.int32) // CAP
    live_stack = stack_offsets(near_live[:, :, None], F_DEV, F_DEV)[:, :, 0]
    reach = device * F_DEV + frame_local[:, None] - offsets[None, :] >= 0
    within = offsets[None, None, :] <= windows[:, None, None]
    anchor_ok = device * F_DEV + frame_local[None, :] - windows[:, None] > 0
    anchor_live = slot_index < counts[0]
    visible = jnp.concatenate(
        [(live_stack & reach)[None] & within, anchor_ok[:, :, None] & anchor_live[None, None, :]],
        axis=2,
    )

    def per_head(items):
        q_head, g_head, k_head, v_head, seen = items
        return attend(q_head, g_head, k_head, v_head, seen, row_live)

    q_heads = to_heads(q_norm.reshape(F_DEV, CAP, local_width))
    g_heads = to_heads(grad_mask.reshape(F_DEV, CAP, local_width))
    attn_h, lse_h, delta_h, grad_qh, grad_kh, grad_vh = lax.map(
        per_head, (q_heads, g_heads, to_heads(k_set), to_heads(v_set), visible)
    )
    attn_out = from_heads(attn_h).reshape(row_count, local_width)
    grad_qn = from_heads(grad_qh).reshape(row_count, local_width)
    grad_k_all = from_heads(grad_kh)
    grad_v_all = from_heads(grad_vh)
    split = (F_DEV + 1) * CAP
    grad_k_near = fold_offsets(grad_k_all[:, :split], F_DEV, F_DEV, CAP)
    grad_v_near = fold_offsets(grad_v_all[:, :split], F_DEV, F_DEV, CAP)
    grad_k_anchor = jnp.sum(grad_k_all[:, split:], axis=0)
    grad_v_anchor = jnp.sum(grad_v_all[:, split:], axis=0)
    back_k, back_v = shifted(jnp.stack([grad_k_near[:F_DEV], grad_v_near[:F_DEV]]), "seq", -1)
    grad_k_own = grad_k_near[F_DEV:] + back_k
    grad_v_own = grad_v_near[F_DEV:] + back_v
    anchor_gk, anchor_gv = tree_reduce(jnp.stack([grad_k_anchor, grad_v_anchor]), "seq", jnp.bfloat16)
    first_device = device == 0
    grad_k_own = grad_k_own.at[0].add(jnp.where(first_device, anchor_gk, 0.0))
    grad_v_own = grad_v_own.at[0].add(jnp.where(first_device, anchor_gv, 0.0))
    q_scaled = grad_qn * q_gain
    k_scaled = grad_k_own.reshape(row_count, local_width) * k_gain
    q_dot, k_dot = xor_psum(
        jnp.stack([jnp.sum(q_float * q_scaled, axis=1), jnp.sum(k_float * k_scaled, axis=1)]), "tp"
    )
    grad_q = (q_rinv * q_scaled - q_float * q_rinv**3 * q_dot[:, None] / WIDTH).astype(jnp.bfloat16)
    grad_k = (k_rinv * k_scaled - k_float * k_rinv**3 * k_dot[:, None] / WIDTH).astype(jnp.bfloat16)
    grad_v = grad_v_own.reshape(row_count, local_width).astype(jnp.bfloat16)
    return (attn_out, grad_q, grad_k, grad_v)


def solution(mesh):
    return jax.shard_map(
        on_device,
        mesh=mesh,
        in_specs=(
            P("seq", "tp"),
            P("seq", "tp"),
            P("seq", "tp"),
            P("tp"),
            P("tp"),
            P("seq", "tp"),
            P(),
            P("tp"),
        ),
        out_specs=(P("seq", "tp"), P("seq", "tp"), P("seq", "tp"), P("seq", "tp")),
        check_vma=False,
    )
```

```python
import jax
import jax.numpy as jnp
from jax import lax
from jax.sharding import PartitionSpec as P

HD = 128
CAP = 256
F_DEV = 2
WIDTH = 4096


EPS = 1e-06
NEG = -1e30


def shifted(block, axis, distance):
    devices = range(lax.axis_size(axis))
    route = [(i - distance, i) for i in devices if i - distance in devices]
    return lax.ppermute(block, axis, route)


def gather_sum(values, axis):
    n = lax.axis_size(axis)
    copies = jnp.broadcast_to(values[None], (n,) + values.shape)
    return jnp.sum(lax.all_to_all(copies, axis, 0, 0, tiled=False), axis=0)


def tree_plan(n):
    fans, m = [], n
    if m % 2 == 0 and (m.bit_length() - 1) % 2 == 1 and m & (m - 1) == 0:
        fans.append(2)
        m //= 2
    while m > 1:
        f = 4 if m % 4 == 0 else next(p for p in range(2, m + 1) if m % p == 0)
        fans.append(f)
        m //= f
    plan, step = [], 1
    for f in fans:
        plan.append((step, f))
        step *= f
    return plan


def tree_bcast(values, axis):
    n = lax.axis_size(axis)
    me = lax.axis_index(axis)
    for step, fan in reversed(tree_plan(n)):
        span = step * fan
        got = values
        for j in range(1, fan):
            route = [(i, i + j * step) for i in range(0, n, span) if i + j * step < n]
            arrived = lax.ppermute(values, axis, route)
            hit = me % span == j * step
            got = jax.tree.map(lambda a, g: jnp.where(hit, a, g), arrived, got)
        values = got
    return values


def tree_reduce(values, axis, wire):
    n = lax.axis_size(axis)
    for step, fan in tree_plan(n):
        span = step * fan
        total = values
        for j in range(1, fan):
            route = [(i + j * step, i) for i in range(0, n, span) if i + j * step < n]
            sent = jax.tree.map(lambda a: a.astype(wire), values)
            arrived = lax.ppermute(sent, axis, route)
            total = jax.tree.map(lambda t, a: t + a.astype(t.dtype), total, arrived)
        values = total
    return values


def stack_offsets(padded, before, count):
    blocks = [padded[before - offset : before - offset + count] for offset in range(before + 1)]
    return jnp.concatenate(blocks, axis=1)


def fold_offsets(grads, before, count, slots):
    result = jnp.zeros((before + count, slots) + grads.shape[2:], jnp.float32)
    for offset in range(before + 1):
        piece = grads[:, offset * slots : (offset + 1) * slots]
        result = result + jnp.pad(piece, ((before - offset, offset), (0, 0), (0, 0)))
    return result


def attend(q_head, g_head, k_set, v_set, visible, row_live):
    factor = HD ** (-0.5)
    scores = jnp.einsum("fqd,fkd->fqk", q_head, k_set, preferred_element_type=jnp.float32) * factor
    scores = jnp.where(visible[:, None, :], scores, NEG)
    row_max = jnp.max(scores, axis=2, keepdims=True)
    row_sum = jnp.sum(jnp.exp(scores - row_max), axis=2, keepdims=True)
    lse = row_max + jnp.log(row_sum)
    prob_wide = jnp.exp(scores - lse)
    prob = prob_wide.astype(jnp.bfloat16)
    out_wide = jnp.einsum("fqk,fkd->fqd", prob, v_set, preferred_element_type=jnp.float32)
    attn = lax.optimization_barrier(
        jnp.where(row_live[:, :, None], out_wide, 0.0).astype(jnp.bfloat16)
    )
    delta = jnp.sum(g_head.astype(jnp.float32) * attn.astype(jnp.float32), axis=2)
    dprob = jnp.einsum("fqd,fkd->fqk", g_head, v_set, preferred_element_type=jnp.float32)
    dscore = (prob_wide * (dprob - delta[:, :, None]) * factor).astype(jnp.bfloat16)
    grad_qh = jnp.einsum("fqk,fkd->fqd", dscore, k_set, preferred_element_type=jnp.float32)
    grad_kh = jnp.einsum("fqk,fqd->fkd", dscore, q_head, preferred_element_type=jnp.float32)
    grad_vh = jnp.einsum("fqk,fqd->fkd", prob, g_head, preferred_element_type=jnp.float32)
    return (attn, lse[:, :, 0], delta, grad_qh, grad_kh, grad_vh)


def on_device(q_in, k_in, v_in, q_gain, k_gain, d_out, counts, windows):
    row_count, local_width = q_in.shape
    local_heads = local_width // HD
    device = lax.axis_index("seq")
    q_float = q_in.astype(jnp.float32)
    k_float = k_in.astype(jnp.float32)
    q_power, k_power = gather_sum(
        jnp.stack([jnp.sum(q_float * q_float, axis=1), jnp.sum(k_float * k_float, axis=1)]), "tp"
    )
    q_rinv = lax.rsqrt(q_power / WIDTH + EPS)[:, None]
    k_rinv = lax.rsqrt(k_power / WIDTH + EPS)[:, None]
    q_norm = (q_float * q_rinv * q_gain).astype(jnp.bfloat16)
    k_norm = (k_float * k_rinv * k_gain).astype(jnp.bfloat16)
    padded_counts = jnp.concatenate([jnp.zeros((F_DEV,), jnp.int32), counts])
    near_counts = lax.dynamic_slice_in_dim(padded_counts, device * F_DEV, 2 * F_DEV)
    slot_index = jnp.arange(CAP, dtype=jnp.int32)
    near_live = slot_index[None, :] < near_counts[:, None]
    row_live = near_live[F_DEV:]
    grad_mask = jnp.where(row_live.reshape(row_count)[:, None], d_out, jnp.zeros_like(d_out))
    halo_k, halo_v = shifted(jnp.stack([k_norm, v_in]), "seq", 1)
    anchor_k, anchor_v = tree_bcast(jnp.stack([k_norm[:CAP], v_in[:CAP]]), "seq")
    k_near = jnp.concatenate([halo_k, k_norm], axis=0).reshape(2 * F_DEV, CAP, local_width)
    v_near = jnp.concatenate([halo_v, v_in], axis=0).reshape(2 * F_DEV, CAP, local_width)
    k_set = jnp.concatenate(
        [
            stack_offsets(k_near, F_DEV, F_DEV),
            jnp.broadcast_to(anchor_k[None], (F_DEV, CAP, local_width)),
        ],
        axis=1,
    )
    v_set = jnp.concatenate(
        [
            stack_offsets(v_near, F_DEV, F_DEV),
            jnp.broadcast_to(anchor_v[None], (F_DEV, CAP, local_width)),
        ],
        axis=1,
    )

    def to_heads(value):
        return value.reshape(value.shape[0], value.shape[1], local_heads, HD).transpose(2, 0, 1, 3)

    def from_heads(value):
        return value.transpose(1, 2, 0, 3).reshape(value.shape[1], value.shape[2], local_heads * HD)

    frame_local = jnp.arange(F_DEV, dtype=jnp.int32)
    offsets = jnp.arange((F_DEV + 1) * CAP, dtype=jnp.int32) // CAP
    live_stack = stack_offsets(near_live[:, :, None], F_DEV, F_DEV)[:, :, 0]
    reach = device * F_DEV + frame_local[:, None] - offsets[None, :] >= 0
    within = offsets[None, None, :] <= windows[:, None, None]
    anchor_ok = device * F_DEV + frame_local[None, :] - windows[:, None] > 0
    anchor_live = slot_index < counts[0]
    visible = jnp.concatenate(
        [(live_stack & reach)[None] & within, anchor_ok[:, :, None] & anchor_live[None, None, :]],
        axis=2,
    )

    def per_head(items):
        q_head, g_head, k_head, v_head, seen = items
        return attend(q_head, g_head, k_head, v_head, seen, row_live)

    q_heads = to_heads(q_norm.reshape(F_DEV, CAP, local_width))
    g_heads = to_heads(grad_mask.reshape(F_DEV, CAP, local_width))
    attn_h, lse_h, delta_h, grad_qh, grad_kh, grad_vh = lax.map(
        per_head, (q_heads, g_heads, to_heads(k_set), to_heads(v_set), visible)
    )
    attn_out = from_heads(attn_h).reshape(row_count, local_width)
    grad_qn = from_heads(grad_qh).reshape(row_count, local_width)
    grad_k_all = from_heads(grad_kh)
    grad_v_all = from_heads(grad_vh)
    split = (F_DEV + 1) * CAP
    grad_k_near = fold_offsets(grad_k_all[:, :split], F_DEV, F_DEV, CAP)
    grad_v_near = fold_offsets(grad_v_all[:, :split], F_DEV, F_DEV, CAP)
    grad_k_anchor = jnp.sum(grad_k_all[:, split:], axis=0)
    grad_v_anchor = jnp.sum(grad_v_all[:, split:], axis=0)
    back_k, back_v = shifted(jnp.stack([grad_k_near[:F_DEV], grad_v_near[:F_DEV]]), "seq", -1)
    grad_k_own = grad_k_near[F_DEV:] + back_k
    grad_v_own = grad_v_near[F_DEV:] + back_v
    anchor_gk, anchor_gv = tree_reduce(jnp.stack([grad_k_anchor, grad_v_anchor]), "seq", jnp.bfloat16)
    first_device = device == 0
    grad_k_own = grad_k_own.at[0].add(jnp.where(first_device, anchor_gk, 0.0))
    grad_v_own = grad_v_own.at[0].add(jnp.where(first_device, anchor_gv, 0.0))
    q_scaled = grad_qn * q_gain
    k_scaled = grad_k_own.reshape(row_count, local_width) * k_gain
    q_dot, k_dot = gather_sum(
        jnp.stack([jnp.sum(q_float * q_scaled, axis=1), jnp.sum(k_float * k_scaled, axis=1)]), "tp"
    )
    grad_q = (q_rinv * q_scaled - q_float * q_rinv**3 * q_dot[:, None] / WIDTH).astype(jnp.bfloat16)
    grad_k = (k_rinv * k_scaled - k_float * k_rinv**3 * k_dot[:, None] / WIDTH).astype(jnp.bfloat16)
    grad_v = grad_v_own.reshape(row_count, local_width).astype(jnp.bfloat16)
    return (attn_out, grad_q, grad_k, grad_v)


def solution(mesh):
    return jax.shard_map(
        on_device,
        mesh=mesh,
        in_specs=(
            P("seq", "tp"),
            P("seq", "tp"),
            P("seq", "tp"),
            P("tp"),
            P("tp"),
            P("seq", "tp"),
            P(),
            P("tp"),
        ),
        out_specs=(P("seq", "tp"), P("seq", "tp"), P("seq", "tp"), P("seq", "tp")),
        check_vma=False,
    )
```

```python
import jax
import jax.numpy as jnp
from jax import lax
from jax.sharding import PartitionSpec as P

HD = 128
CAP = 256
F_DEV = 2
WIDTH = 4096


EPS = 1e-06
NEG = -1e30


def shifted(block, axis, distance):
    devices = range(lax.axis_size(axis))
    route = [(i - distance, i) for i in devices if i - distance in devices]
    return lax.ppermute(block, axis, route)


def gather_sum(values, axis):
    n = lax.axis_size(axis)
    copies = jnp.broadcast_to(values[None], (n,) + values.shape)
    return jnp.sum(lax.all_to_all(copies, axis, 0, 0, tiled=False), axis=0)


def tree_plan(n):
    fans, m = [], n
    if m % 2 == 0 and (m.bit_length() - 1) % 2 == 1 and m & (m - 1) == 0:
        fans.append(2)
        m //= 2
    while m > 1:
        f = 4 if m % 4 == 0 else next(p for p in range(2, m + 1) if m % p == 0)
        fans.append(f)
        m //= f
    plan, step = [], 1
    for f in fans:
        plan.append((step, f))
        step *= f
    return plan


def tree_bcast(values, axis):
    n = lax.axis_size(axis)
    me = lax.axis_index(axis)
    for step, fan in reversed(tree_plan(n)):
        span = step * fan
        got = values
        for j in range(1, fan):
            route = [(i, i + j * step) for i in range(0, n, span) if i + j * step < n]
            arrived = lax.ppermute(values, axis, route)
            hit = me % span == j * step
            got = jax.tree.map(lambda a, g: jnp.where(hit, a, g), arrived, got)
        values = got
    return values


def tree_reduce(values, axis, wire):
    n = lax.axis_size(axis)
    for step, fan in tree_plan(n):
        span = step * fan
        total = values
        for j in range(1, fan):
            route = [(i + j * step, i) for i in range(0, n, span) if i + j * step < n]
            sent = jax.tree.map(lambda a: a.astype(wire), values)
            arrived = lax.ppermute(sent, axis, route)
            total = jax.tree.map(lambda t, a: t + a.astype(t.dtype), total, arrived)
        values = total
    return values


def stack_offsets(padded, before, count):
    blocks = [padded[before - offset : before - offset + count] for offset in range(before + 1)]
    return jnp.concatenate(blocks, axis=1)


def fold_offsets(grads, before, count, slots):
    result = jnp.zeros((before + count, slots) + grads.shape[2:], jnp.float32)
    for offset in range(before + 1):
        piece = grads[:, offset * slots : (offset + 1) * slots]
        result = result + jnp.pad(piece, ((before - offset, offset), (0, 0), (0, 0)))
    return result


def attend_split(q, g, k_win, v_win, k_anc, v_anc, seen_win, seen_anc, row_live):
    factor = HD ** (-0.5)
    wide = jnp.float32
    s_win = jnp.einsum("hfqd,hfkd->hfqk", q, k_win, preferred_element_type=wide) * factor
    s_anc = jnp.einsum("hfqd,hkd->hfqk", q, k_anc, preferred_element_type=wide) * factor
    s_win = jnp.where(seen_win[:, :, None, :], s_win, NEG)
    s_anc = jnp.where(seen_anc[:, :, None, :], s_anc, NEG)
    row_max = jnp.maximum(
        jnp.max(s_win, axis=3, keepdims=True), jnp.max(s_anc, axis=3, keepdims=True)
    )
    row_sum = jnp.sum(jnp.exp(s_win - row_max), axis=3, keepdims=True) + jnp.sum(
        jnp.exp(s_anc - row_max), axis=3, keepdims=True
    )
    lse = row_max + jnp.log(row_sum)
    p_win = jnp.exp(s_win - lse)
    p_anc = jnp.exp(s_anc - lse)
    pb_win = p_win.astype(jnp.bfloat16)
    pb_anc = p_anc.astype(jnp.bfloat16)
    out = jnp.einsum("hfqk,hfkd->hfqd", pb_win, v_win, preferred_element_type=wide) + jnp.einsum(
        "hfqk,hkd->hfqd", pb_anc, v_anc, preferred_element_type=wide
    )
    attn = lax.optimization_barrier(
        jnp.where(row_live[None, :, :, None], out, 0.0).astype(jnp.bfloat16)
    )
    delta = jnp.sum(g.astype(wide) * attn.astype(wide), axis=3, keepdims=True)
    dp_win = jnp.einsum("hfqd,hfkd->hfqk", g, v_win, preferred_element_type=wide)
    dp_anc = jnp.einsum("hfqd,hkd->hfqk", g, v_anc, preferred_element_type=wide)
    ds_win = (p_win * (dp_win - delta) * factor).astype(jnp.bfloat16)
    ds_anc = (p_anc * (dp_anc - delta) * factor).astype(jnp.bfloat16)
    gk_anc = jnp.einsum("hfqk,hfqd->hkd", ds_anc, q, preferred_element_type=wide)
    gv_anc = jnp.einsum("hfqk,hfqd->hkd", pb_anc, g, preferred_element_type=wide)
    gq = jnp.einsum("hfqk,hfkd->hfqd", ds_win, k_win, preferred_element_type=wide) + jnp.einsum(
        "hfqk,hkd->hfqd", ds_anc, k_anc, preferred_element_type=wide
    )
    gk_win = jnp.einsum("hfqk,hfqd->hfkd", ds_win, q, preferred_element_type=wide)
    gv_win = jnp.einsum("hfqk,hfqd->hfkd", pb_win, g, preferred_element_type=wide)
    return attn, gq, gk_win, gv_win, gk_anc, gv_anc


def on_device(q_in, k_in, v_in, q_gain, k_gain, d_out, counts, windows):
    row_count, local_width = q_in.shape
    local_heads = local_width // HD
    device = lax.axis_index("seq")
    q_float = q_in.astype(jnp.float32)
    k_float = k_in.astype(jnp.float32)
    q_power, k_power = gather_sum(
        jnp.stack([jnp.sum(q_float * q_float, axis=1), jnp.sum(k_float * k_float, axis=1)]), "tp"
    )
    q_rinv = lax.rsqrt(q_power / WIDTH + EPS)[:, None]
    k_rinv = lax.rsqrt(k_power / WIDTH + EPS)[:, None]
    q_norm = (q_float * q_rinv * q_gain).astype(jnp.bfloat16)
    k_norm = (k_float * k_rinv * k_gain).astype(jnp.bfloat16)
    padded_counts = jnp.concatenate([jnp.zeros((F_DEV,), jnp.int32), counts])
    near_counts = lax.dynamic_slice_in_dim(padded_counts, device * F_DEV, 2 * F_DEV)
    slot_index = jnp.arange(CAP, dtype=jnp.int32)
    near_live = slot_index[None, :] < near_counts[:, None]
    row_live = near_live[F_DEV:]
    grad_mask = jnp.where(row_live.reshape(row_count)[:, None], d_out, jnp.zeros_like(d_out))
    halo_k, halo_v = shifted(jnp.stack([k_norm, v_in]), "seq", 1)
    anchor_k, anchor_v = tree_bcast(jnp.stack([k_norm[:CAP], v_in[:CAP]]), "seq")
    k_near = jnp.concatenate([halo_k, k_norm], axis=0).reshape(2 * F_DEV, CAP, local_width)
    v_near = jnp.concatenate([halo_v, v_in], axis=0).reshape(2 * F_DEV, CAP, local_width)
    def to_heads(value):
        return value.reshape(value.shape[0], value.shape[1], local_heads, HD).transpose(2, 0, 1, 3)

    def from_heads(value):
        return value.transpose(1, 2, 0, 3).reshape(value.shape[1], value.shape[2], local_heads * HD)

    def rows_to_heads(value):
        return value.reshape(value.shape[0], local_heads, HD).transpose(1, 0, 2)

    frame_local = jnp.arange(F_DEV, dtype=jnp.int32)
    offsets = jnp.arange((F_DEV + 1) * CAP, dtype=jnp.int32) // CAP
    live_stack = stack_offsets(near_live[:, :, None], F_DEV, F_DEV)[:, :, 0]
    reach = device * F_DEV + frame_local[:, None] - offsets[None, :] >= 0
    within = offsets[None, None, :] <= windows[:, None, None]
    anchor_ok = device * F_DEV + frame_local[None, :] - windows[:, None] > 0
    anchor_live = slot_index < counts[0]
    seen_win = (live_stack & reach)[None] & within
    seen_anc = anchor_ok[:, :, None] & anchor_live[None, None, :]

    q_heads = to_heads(q_norm.reshape(F_DEV, CAP, local_width))
    g_heads = to_heads(grad_mask.reshape(F_DEV, CAP, local_width))
    attn_h, grad_qh, grad_kh, grad_vh, grad_ka, grad_va = attend_split(
        q_heads,
        g_heads,
        to_heads(stack_offsets(k_near, F_DEV, F_DEV)),
        to_heads(stack_offsets(v_near, F_DEV, F_DEV)),
        rows_to_heads(anchor_k),
        rows_to_heads(anchor_v),
        seen_win,
        seen_anc,
        row_live,
    )
    attn_out = from_heads(attn_h).reshape(row_count, local_width)
    grad_qn = from_heads(grad_qh).reshape(row_count, local_width)
    grad_k_near = fold_offsets(from_heads(grad_kh), F_DEV, F_DEV, CAP)
    grad_v_near = fold_offsets(from_heads(grad_vh), F_DEV, F_DEV, CAP)
    grad_k_anchor = grad_ka.transpose(1, 0, 2).reshape(CAP, local_width)
    grad_v_anchor = grad_va.transpose(1, 0, 2).reshape(CAP, local_width)
    back_k, back_v = shifted(jnp.stack([grad_k_near[:F_DEV], grad_v_near[:F_DEV]]), "seq", -1)
    grad_k_own = grad_k_near[F_DEV:] + back_k
    grad_v_own = grad_v_near[F_DEV:] + back_v
    anchor_gk, anchor_gv = tree_reduce(jnp.stack([grad_k_anchor, grad_v_anchor]), "seq", jnp.bfloat16)
    first_device = device == 0
    grad_k_own = grad_k_own.at[0].add(jnp.where(first_device, anchor_gk, 0.0))
    grad_v_own = grad_v_own.at[0].add(jnp.where(first_device, anchor_gv, 0.0))
    q_scaled = grad_qn * q_gain
    k_scaled = grad_k_own.reshape(row_count, local_width) * k_gain
    q_dot, k_dot = gather_sum(
        jnp.stack([jnp.sum(q_float * q_scaled, axis=1), jnp.sum(k_float * k_scaled, axis=1)]), "tp"
    )
    grad_q = (q_rinv * q_scaled - q_float * q_rinv**3 * q_dot[:, None] / WIDTH).astype(jnp.bfloat16)
    grad_k = (k_rinv * k_scaled - k_float * k_rinv**3 * k_dot[:, None] / WIDTH).astype(jnp.bfloat16)
    grad_v = grad_v_own.reshape(row_count, local_width).astype(jnp.bfloat16)
    return (attn_out, grad_q, grad_k, grad_v)


def solution(mesh):
    return jax.shard_map(
        on_device,
        mesh=mesh,
        in_specs=(
            P("seq", "tp"),
            P("seq", "tp"),
            P("seq", "tp"),
            P("tp"),
            P("tp"),
            P("seq", "tp"),
            P(),
            P("tp"),
        ),
        out_specs=(P("seq", "tp"), P("seq", "tp"), P("seq", "tp"), P("seq", "tp")),
        check_vma=False,
    )
```

```python
import functools

import jax
import jax.numpy as jnp
from jax import lax
from jax.sharding import PartitionSpec as P

HD = 128
CAP = 256
F_DEV = 2
WIDTH = 4096


EPS = 1e-06
NEG = -1e30


def shifted(block, axis, distance):
    devices = range(lax.axis_size(axis))
    route = [(i - distance, i) for i in devices if i - distance in devices]
    return lax.ppermute(block, axis, route)


def gather_sum(values, axis):
    n = lax.axis_size(axis)
    copies = jnp.broadcast_to(values[None], (n,) + values.shape)
    return jnp.sum(lax.all_to_all(copies, axis, 0, 0, tiled=False), axis=0)


def tree_plan(n):
    fans, m = [], n
    if m % 2 == 0 and (m.bit_length() - 1) % 2 == 1 and m & (m - 1) == 0:
        fans.append(2)
        m //= 2
    while m > 1:
        f = 4 if m % 4 == 0 else next(p for p in range(2, m + 1) if m % p == 0)
        fans.append(f)
        m //= f
    plan, step = [], 1
    for f in fans:
        plan.append((step, f))
        step *= f
    return plan[::-1]


def digit(i, step, fan):
    return (i // step) % fan


def tree_rounds(n):
    done = []
    for step, fan in tree_plan(n):
        base = [i for i in range(n) if digit(i, step, fan) == 0 and all(digit(i, s, f) == 0 for s, f in done)]
        yield step, fan, list(done), base
        done.append((step, fan))


def tree_bcast(values, axis):
    n = lax.axis_size(axis)
    me = lax.axis_index(axis)
    for step, fan, done, base in reversed(list(tree_rounds(n))):
        clear = functools.reduce(
            lambda acc, sf: acc & (digit(me, *sf) == 0), done, jnp.bool_(True)
        )
        got = values
        for j in range(1, fan):
            route = [(i, i + j * step) for i in base if i + j * step < n]
            arrived = lax.ppermute(values, axis, route)
            hit = clear & (digit(me, step, fan) == j)
            got = jax.tree.map(lambda a, g: jnp.where(hit, a, g), arrived, got)
        values = got
    return values


def tree_reduce(values, axis, wire):
    n = lax.axis_size(axis)
    for step, fan, done, base in tree_rounds(n):
        total = values
        for j in range(1, fan):
            route = [(i + j * step, i) for i in base if i + j * step < n]
            sent = jax.tree.map(lambda a: a.astype(wire), values)
            arrived = lax.ppermute(sent, axis, route)
            total = jax.tree.map(lambda t, a: t + a.astype(t.dtype), total, arrived)
        values = total
    return values


def stack_offsets(padded, before, count):
    blocks = [padded[before - offset : before - offset + count] for offset in range(before + 1)]
    return jnp.concatenate(blocks, axis=1)


def fold_offsets(grads, before, count, slots):
    result = jnp.zeros((before + count, slots) + grads.shape[2:], jnp.float32)
    for offset in range(before + 1):
        piece = grads[:, offset * slots : (offset + 1) * slots]
        result = result + jnp.pad(piece, ((before - offset, offset), (0, 0), (0, 0)))
    return result


def attend_split(q, g, k_win, v_win, k_anc, v_anc, seen_win, seen_anc, row_live):
    factor = HD ** (-0.5)
    wide = jnp.float32
    s_win = jnp.einsum("hfqd,hfkd->hfqk", q, k_win, preferred_element_type=wide) * factor
    s_anc = jnp.einsum("hfqd,hkd->hfqk", q, k_anc, preferred_element_type=wide) * factor
    s_win = jnp.where(seen_win[:, :, None, :], s_win, NEG)
    s_anc = jnp.where(seen_anc[:, :, None, :], s_anc, NEG)
    row_max = jnp.maximum(
        jnp.max(s_win, axis=3, keepdims=True), jnp.max(s_anc, axis=3, keepdims=True)
    )
    row_sum = jnp.sum(jnp.exp(s_win - row_max), axis=3, keepdims=True) + jnp.sum(
        jnp.exp(s_anc - row_max), axis=3, keepdims=True
    )
    lse = row_max + jnp.log(row_sum)
    p_win = jnp.exp(s_win - lse)
    p_anc = jnp.exp(s_anc - lse)
    pb_win = p_win.astype(jnp.bfloat16)
    pb_anc = p_anc.astype(jnp.bfloat16)
    out = jnp.einsum("hfqk,hfkd->hfqd", pb_win, v_win, preferred_element_type=wide) + jnp.einsum(
        "hfqk,hkd->hfqd", pb_anc, v_anc, preferred_element_type=wide
    )
    attn = lax.optimization_barrier(
        jnp.where(row_live[None, :, :, None], out, 0.0).astype(jnp.bfloat16)
    )
    delta = jnp.sum(g.astype(wide) * attn.astype(wide), axis=3, keepdims=True)
    dp_win = jnp.einsum("hfqd,hfkd->hfqk", g, v_win, preferred_element_type=wide)
    dp_anc = jnp.einsum("hfqd,hkd->hfqk", g, v_anc, preferred_element_type=wide)
    ds_win = (p_win * (dp_win - delta) * factor).astype(jnp.bfloat16)
    ds_anc = (p_anc * (dp_anc - delta) * factor).astype(jnp.bfloat16)
    gk_anc = jnp.einsum("hfqk,hfqd->hkd", ds_anc, q, preferred_element_type=wide)
    gv_anc = jnp.einsum("hfqk,hfqd->hkd", pb_anc, g, preferred_element_type=wide)
    gq = jnp.einsum("hfqk,hfkd->hfqd", ds_win, k_win, preferred_element_type=wide) + jnp.einsum(
        "hfqk,hkd->hfqd", ds_anc, k_anc, preferred_element_type=wide
    )
    gk_win = jnp.einsum("hfqk,hfqd->hfkd", ds_win, q, preferred_element_type=wide)
    gv_win = jnp.einsum("hfqk,hfqd->hfkd", pb_win, g, preferred_element_type=wide)
    return attn, gq, gk_win, gv_win, gk_anc, gv_anc


def on_device(q_in, k_in, v_in, q_gain, k_gain, d_out, counts, windows):
    row_count, local_width = q_in.shape
    local_heads = local_width // HD
    device = lax.axis_index("seq")
    q_float = q_in.astype(jnp.float32)
    k_float = k_in.astype(jnp.float32)
    q_power, k_power = gather_sum(
        jnp.stack([jnp.sum(q_float * q_float, axis=1), jnp.sum(k_float * k_float, axis=1)]), "tp"
    )
    q_rinv = lax.rsqrt(q_power / WIDTH + EPS)[:, None]
    k_rinv = lax.rsqrt(k_power / WIDTH + EPS)[:, None]
    q_norm = (q_float * q_rinv * q_gain).astype(jnp.bfloat16)
    k_norm = (k_float * k_rinv * k_gain).astype(jnp.bfloat16)
    padded_counts = jnp.concatenate([jnp.zeros((F_DEV,), jnp.int32), counts])
    near_counts = lax.dynamic_slice_in_dim(padded_counts, device * F_DEV, 2 * F_DEV)
    slot_index = jnp.arange(CAP, dtype=jnp.int32)
    near_live = slot_index[None, :] < near_counts[:, None]
    row_live = near_live[F_DEV:]
    grad_mask = jnp.where(row_live.reshape(row_count)[:, None], d_out, jnp.zeros_like(d_out))
    halo_k, halo_v = shifted(jnp.stack([k_norm, v_in]), "seq", 1)
    anchor_k, anchor_v = tree_bcast(jnp.stack([k_norm[:CAP], v_in[:CAP]]), "seq")
    k_near = jnp.concatenate([halo_k, k_norm], axis=0).reshape(2 * F_DEV, CAP, local_width)
    v_near = jnp.concatenate([halo_v, v_in], axis=0).reshape(2 * F_DEV, CAP, local_width)
    def to_heads(value):
        return value.reshape(value.shape[0], value.shape[1], local_heads, HD).transpose(2, 0, 1, 3)

    def from_heads(value):
        return value.transpose(1, 2, 0, 3).reshape(value.shape[1], value.shape[2], local_heads * HD)

    def rows_to_heads(value):
        return value.reshape(value.shape[0], local_heads, HD).transpose(1, 0, 2)

    frame_local = jnp.arange(F_DEV, dtype=jnp.int32)
    offsets = jnp.arange((F_DEV + 1) * CAP, dtype=jnp.int32) // CAP
    live_stack = stack_offsets(near_live[:, :, None], F_DEV, F_DEV)[:, :, 0]
    reach = device * F_DEV + frame_local[:, None] - offsets[None, :] >= 0
    within = offsets[None, None, :] <= windows[:, None, None]
    anchor_ok = device * F_DEV + frame_local[None, :] - windows[:, None] > 0
    anchor_live = slot_index < counts[0]
    seen_win = (live_stack & reach)[None] & within
    seen_anc = anchor_ok[:, :, None] & anchor_live[None, None, :]

    q_heads = to_heads(q_norm.reshape(F_DEV, CAP, local_width))
    g_heads = to_heads(grad_mask.reshape(F_DEV, CAP, local_width))
    attn_h, grad_qh, grad_kh, grad_vh, grad_ka, grad_va = attend_split(
        q_heads,
        g_heads,
        to_heads(stack_offsets(k_near, F_DEV, F_DEV)),
        to_heads(stack_offsets(v_near, F_DEV, F_DEV)),
        rows_to_heads(anchor_k),
        rows_to_heads(anchor_v),
        seen_win,
        seen_anc,
        row_live,
    )
    attn_out = from_heads(attn_h).reshape(row_count, local_width)
    grad_qn = from_heads(grad_qh).reshape(row_count, local_width)
    grad_k_near = fold_offsets(from_heads(grad_kh), F_DEV, F_DEV, CAP)
    grad_v_near = fold_offsets(from_heads(grad_vh), F_DEV, F_DEV, CAP)
    grad_k_anchor = grad_ka.transpose(1, 0, 2).reshape(CAP, local_width)
    grad_v_anchor = grad_va.transpose(1, 0, 2).reshape(CAP, local_width)
    back_k, back_v = shifted(jnp.stack([grad_k_near[:F_DEV], grad_v_near[:F_DEV]]), "seq", -1)
    grad_k_own = grad_k_near[F_DEV:] + back_k
    grad_v_own = grad_v_near[F_DEV:] + back_v
    anchor_gk, anchor_gv = tree_reduce(jnp.stack([grad_k_anchor, grad_v_anchor]), "seq", jnp.bfloat16)
    first_device = device == 0
    grad_k_own = grad_k_own.at[0].add(jnp.where(first_device, anchor_gk, 0.0))
    grad_v_own = grad_v_own.at[0].add(jnp.where(first_device, anchor_gv, 0.0))
    q_scaled = grad_qn * q_gain
    k_scaled = grad_k_own.reshape(row_count, local_width) * k_gain
    q_dot, k_dot = gather_sum(
        jnp.stack([jnp.sum(q_float * q_scaled, axis=1), jnp.sum(k_float * k_scaled, axis=1)]), "tp"
    )
    grad_q = (q_rinv * q_scaled - q_float * q_rinv**3 * q_dot[:, None] / WIDTH).astype(jnp.bfloat16)
    grad_k = (k_rinv * k_scaled - k_float * k_rinv**3 * k_dot[:, None] / WIDTH).astype(jnp.bfloat16)
    grad_v = grad_v_own.reshape(row_count, local_width).astype(jnp.bfloat16)
    return (attn_out, grad_q, grad_k, grad_v)


def solution(mesh):
    return jax.shard_map(
        on_device,
        mesh=mesh,
        in_specs=(
            P("seq", "tp"),
            P("seq", "tp"),
            P("seq", "tp"),
            P("tp"),
            P("tp"),
            P("seq", "tp"),
            P(),
            P("tp"),
        ),
        out_specs=(P("seq", "tp"), P("seq", "tp"), P("seq", "tp"), P("seq", "tp")),
        check_vma=False,
    )
```

```python
import jax
import jax.numpy as jnp
from jax import lax
from jax.sharding import PartitionSpec as P

HD = 128
CAP = 256
F_DEV = 2
WIDTH = 4096


EPS = 1e-06
NEG = -1e30


def shifted(block, axis, distance):
    devices = range(lax.axis_size(axis))
    route = [(i - distance, i) for i in devices if i - distance in devices]
    return lax.ppermute(block, axis, route)


def gather_sum(values, axis):
    n = lax.axis_size(axis)
    copies = jnp.broadcast_to(values[None], (n,) + values.shape)
    return jnp.sum(lax.all_to_all(copies, axis, 0, 0, tiled=False), axis=0)


def tree_plan(n):
    fans, m = [], n
    if m % 2 == 0 and (m.bit_length() - 1) % 2 == 1 and m & (m - 1) == 0:
        fans.append(2)
        m //= 2
    while m > 1:
        f = 4 if m % 4 == 0 else next(p for p in range(2, m + 1) if m % p == 0)
        fans.append(f)
        m //= f
    plan, step = [], 1
    for f in fans:
        plan.append((step, f))
        step *= f
    return plan


def tree_bcast(values, axis):
    n = lax.axis_size(axis)
    me = lax.axis_index(axis)
    for step, fan in reversed(tree_plan(n)):
        span = step * fan
        got = values
        for j in range(1, fan):
            route = [(i, i + j * step) for i in range(0, n, span) if i + j * step < n]
            arrived = lax.ppermute(values, axis, route)
            hit = me % span == j * step
            got = jax.tree.map(lambda a, g: jnp.where(hit, a, g), arrived, got)
        values = got
    return values


def tree_reduce(values, axis, wire, first=0, last=None):
    n = lax.axis_size(axis)
    for step, fan in tree_plan(n)[first:last]:
        span = step * fan
        total = values
        for j in range(1, fan):
            route = [(i + j * step, i) for i in range(0, n, span) if i + j * step < n]
            sent = jax.tree.map(lambda a: a.astype(wire), values)
            arrived = lax.ppermute(sent, axis, route)
            total = jax.tree.map(lambda t, a: t + a.astype(t.dtype), total, arrived)
        values = total
    return values


def stack_offsets(padded, before, count):
    blocks = [padded[before - offset : before - offset + count] for offset in range(before + 1)]
    return jnp.concatenate(blocks, axis=1)


def fold_offsets(grads, before, count, slots):
    result = jnp.zeros((before + count, slots) + grads.shape[2:], jnp.float32)
    for offset in range(before + 1):
        piece = grads[:, offset * slots : (offset + 1) * slots]
        result = result + jnp.pad(piece, ((before - offset, offset), (0, 0), (0, 0)))
    return result


def attend_split(q, g, k_win, v_win, k_anc, v_anc, seen_win, seen_anc, row_live):
    factor = HD ** (-0.5)
    wide = jnp.float32
    s_win = jnp.einsum("hfqd,hfkd->hfqk", q, k_win, preferred_element_type=wide) * factor
    s_anc = jnp.einsum("hfqd,hkd->hfqk", q, k_anc, preferred_element_type=wide) * factor
    s_win = jnp.where(seen_win[:, :, None, :], s_win, NEG)
    s_anc = jnp.where(seen_anc[:, :, None, :], s_anc, NEG)
    row_max = jnp.maximum(
        jnp.max(s_win, axis=3, keepdims=True), jnp.max(s_anc, axis=3, keepdims=True)
    )
    row_sum = jnp.sum(jnp.exp(s_win - row_max), axis=3, keepdims=True) + jnp.sum(
        jnp.exp(s_anc - row_max), axis=3, keepdims=True
    )
    lse = row_max + jnp.log(row_sum)
    p_win = jnp.exp(s_win - lse)
    p_anc = jnp.exp(s_anc - lse)
    pb_win = p_win.astype(jnp.bfloat16)
    pb_anc = p_anc.astype(jnp.bfloat16)
    out = jnp.einsum("hfqk,hfkd->hfqd", pb_win, v_win, preferred_element_type=wide) + jnp.einsum(
        "hfqk,hkd->hfqd", pb_anc, v_anc, preferred_element_type=wide
    )
    attn = lax.optimization_barrier(
        jnp.where(row_live[None, :, :, None], out, 0.0).astype(jnp.bfloat16)
    )
    delta = jnp.sum(g.astype(wide) * attn.astype(wide), axis=3, keepdims=True)
    dp_win = jnp.einsum("hfqd,hfkd->hfqk", g, v_win, preferred_element_type=wide)
    dp_anc = jnp.einsum("hfqd,hkd->hfqk", g, v_anc, preferred_element_type=wide)
    ds_win = (p_win * (dp_win - delta) * factor).astype(jnp.bfloat16)
    ds_anc = (p_anc * (dp_anc - delta) * factor).astype(jnp.bfloat16)
    gk_anc = jnp.einsum("hfqk,hfqd->hkd", ds_anc, q, preferred_element_type=wide)
    gv_anc = jnp.einsum("hfqk,hfqd->hkd", pb_anc, g, preferred_element_type=wide)
    gq = jnp.einsum("hfqk,hfkd->hfqd", ds_win, k_win, preferred_element_type=wide) + jnp.einsum(
        "hfqk,hkd->hfqd", ds_anc, k_anc, preferred_element_type=wide
    )
    gk_win = jnp.einsum("hfqk,hfqd->hfkd", ds_win, q, preferred_element_type=wide)
    gv_win = jnp.einsum("hfqk,hfqd->hfkd", pb_win, g, preferred_element_type=wide)
    return attn, gq, gk_win, gv_win, gk_anc, gv_anc


def on_device(q_in, k_in, v_in, q_gain, k_gain, d_out, counts, windows):
    row_count, local_width = q_in.shape
    local_heads = local_width // HD
    device = lax.axis_index("seq")
    q_float = q_in.astype(jnp.float32)
    k_float = k_in.astype(jnp.float32)
    q_power, k_power = gather_sum(
        jnp.stack([jnp.sum(q_float * q_float, axis=1), jnp.sum(k_float * k_float, axis=1)]), "tp"
    )
    q_rinv = lax.rsqrt(q_power / WIDTH + EPS)[:, None]
    k_rinv = lax.rsqrt(k_power / WIDTH + EPS)[:, None]
    q_norm = (q_float * q_rinv * q_gain).astype(jnp.bfloat16)
    k_norm = (k_float * k_rinv * k_gain).astype(jnp.bfloat16)
    padded_counts = jnp.concatenate([jnp.zeros((F_DEV,), jnp.int32), counts])
    near_counts = lax.dynamic_slice_in_dim(padded_counts, device * F_DEV, 2 * F_DEV)
    slot_index = jnp.arange(CAP, dtype=jnp.int32)
    near_live = slot_index[None, :] < near_counts[:, None]
    row_live = near_live[F_DEV:]
    grad_mask = jnp.where(row_live.reshape(row_count)[:, None], d_out, jnp.zeros_like(d_out))
    halo_k, halo_v = shifted(jnp.stack([k_norm, v_in]), "seq", 1)
    anchor_k, anchor_v = tree_bcast(jnp.stack([k_norm[:CAP], v_in[:CAP]]), "seq")
    k_near = jnp.concatenate([halo_k, k_norm], axis=0).reshape(2 * F_DEV, CAP, local_width)
    v_near = jnp.concatenate([halo_v, v_in], axis=0).reshape(2 * F_DEV, CAP, local_width)
    def to_heads(value):
        return value.reshape(value.shape[0], value.shape[1], local_heads, HD).transpose(2, 0, 1, 3)

    def from_heads(value):
        return value.transpose(1, 2, 0, 3).reshape(value.shape[1], value.shape[2], local_heads * HD)

    def rows_to_heads(value):
        return value.reshape(value.shape[0], local_heads, HD).transpose(1, 0, 2)

    frame_local = jnp.arange(F_DEV, dtype=jnp.int32)
    offsets = jnp.arange((F_DEV + 1) * CAP, dtype=jnp.int32) // CAP
    live_stack = stack_offsets(near_live[:, :, None], F_DEV, F_DEV)[:, :, 0]
    reach = device * F_DEV + frame_local[:, None] - offsets[None, :] >= 0
    within = offsets[None, None, :] <= windows[:, None, None]
    anchor_ok = device * F_DEV + frame_local[None, :] - windows[:, None] > 0
    anchor_live = slot_index < counts[0]
    seen_win = (live_stack & reach)[None] & within
    seen_anc = anchor_ok[:, :, None] & anchor_live[None, None, :]

    q_heads = to_heads(q_norm.reshape(F_DEV, CAP, local_width))
    g_heads = to_heads(grad_mask.reshape(F_DEV, CAP, local_width))
    attn_h, grad_qh, grad_kh, grad_vh, grad_ka, grad_va = attend_split(
        q_heads,
        g_heads,
        to_heads(stack_offsets(k_near, F_DEV, F_DEV)),
        to_heads(stack_offsets(v_near, F_DEV, F_DEV)),
        rows_to_heads(anchor_k),
        rows_to_heads(anchor_v),
        seen_win,
        seen_anc,
        row_live,
    )
    attn_out = from_heads(attn_h).reshape(row_count, local_width)
    grad_qn = from_heads(grad_qh).reshape(row_count, local_width)
    grad_k_near = fold_offsets(from_heads(grad_kh), F_DEV, F_DEV, CAP)
    grad_v_near = fold_offsets(from_heads(grad_vh), F_DEV, F_DEV, CAP)
    grad_k_anchor = grad_ka.transpose(1, 0, 2).reshape(CAP, local_width)
    grad_v_anchor = grad_va.transpose(1, 0, 2).reshape(CAP, local_width)
    back_k, back_v = shifted(jnp.stack([grad_k_near[:F_DEV], grad_v_near[:F_DEV]]), "seq", -1)
    grad_k_own = grad_k_near[F_DEV:] + back_k
    grad_v_own = grad_v_near[F_DEV:] + back_v
    anchor_grads = tree_reduce(
        jnp.stack([grad_k_anchor, grad_v_anchor]), "seq", jnp.bfloat16, last=2
    )
    q_scaled = grad_qn * q_gain
    local_scaled = grad_k_near[F_DEV:].reshape(row_count, local_width) * k_gain
    back_part = jnp.sum(
        halo_k.astype(jnp.float32) * grad_k_near[:F_DEV].reshape(row_count, local_width), axis=1
    )
    anchor_part = jnp.sum(anchor_k.astype(jnp.float32) * grad_k_anchor, axis=1)
    q_dot, local_dot, back_part, anchor_part = gather_sum(
        jnp.stack(
            [
                jnp.sum(q_float * q_scaled, axis=1),
                jnp.sum(k_float * local_scaled, axis=1),
                back_part,
                jnp.pad(anchor_part, (0, row_count - CAP)),
            ]
        ),
        "tp",
    )
    anchor_grads, q_dot, local_dot, back_part, anchor_part = lax.optimization_barrier(
        (anchor_grads, q_dot, local_dot, back_part, anchor_part)
    )
    anchor_gk, anchor_gv = tree_reduce(anchor_grads, "seq", jnp.bfloat16, first=2)
    anchor_part = tree_reduce(anchor_part[:CAP], "seq", jnp.float32)
    back_part = shifted(back_part, "seq", -1)
    first_device = device == 0
    grad_k_own = grad_k_own.at[0].add(jnp.where(first_device, anchor_gk, 0.0))
    grad_v_own = grad_v_own.at[0].add(jnp.where(first_device, anchor_gv, 0.0))
    k_scaled = grad_k_own.reshape(row_count, local_width) * k_gain
    anchor_rows = first_device & (jnp.arange(row_count) < CAP)
    far_part = back_part + jnp.where(anchor_rows, jnp.pad(anchor_part, (0, row_count - CAP)), 0.0)
    k_dot = local_dot + far_part / k_rinv[:, 0]
    grad_q = (q_rinv * q_scaled - q_float * q_rinv**3 * q_dot[:, None] / WIDTH).astype(jnp.bfloat16)
    grad_k = (k_rinv * k_scaled - k_float * k_rinv**3 * k_dot[:, None] / WIDTH).astype(jnp.bfloat16)
    grad_v = grad_v_own.reshape(row_count, local_width).astype(jnp.bfloat16)
    return (attn_out, grad_q, grad_k, grad_v)


def solution(mesh):
    return jax.shard_map(
        on_device,
        mesh=mesh,
        in_specs=(
            P("seq", "tp"),
            P("seq", "tp"),
            P("seq", "tp"),
            P("tp"),
            P("tp"),
            P("seq", "tp"),
            P(),
            P("tp"),
        ),
        out_specs=(P("seq", "tp"), P("seq", "tp"), P("seq", "tp"), P("seq", "tp")),
        check_vma=False,
    )
```

```python
import jax
import jax.numpy as jnp
from jax import lax
from jax.sharding import PartitionSpec as P

HD = 128
CAP = 256
F_DEV = 2
WIDTH = 4096


EPS = 1e-06
NEG = -1e30


def shifted(block, axis, distance):
    devices = range(lax.axis_size(axis))
    route = [(i - distance, i) for i in devices if i - distance in devices]
    return lax.ppermute(block, axis, route)


def gather_sum(values, axis):
    n = lax.axis_size(axis)
    copies = jnp.broadcast_to(values[None], (n,) + values.shape)
    return jnp.sum(lax.all_to_all(copies, axis, 0, 0, tiled=False), axis=0)


def tree_plan(n):
    fans, m = [], n
    if m % 2 == 0 and (m.bit_length() - 1) % 2 == 1 and m & (m - 1) == 0:
        fans.append(2)
        m //= 2
    while m > 1:
        f = 4 if m % 4 == 0 else next(p for p in range(2, m + 1) if m % p == 0)
        fans.append(f)
        m //= f
    plan, step = [], 1
    for f in fans:
        plan.append((step, f))
        step *= f
    return plan


def tree_bcast(values, axis, first=0):
    n = lax.axis_size(axis)
    me = lax.axis_index(axis)
    for step, fan in reversed(tree_plan(n)[first:]):
        span = step * fan
        got = values
        for j in range(1, fan):
            route = [(i, i + j * step) for i in range(0, n, span) if i + j * step < n]
            arrived = lax.ppermute(values, axis, route)
            hit = me % span == j * step
            got = jax.tree.map(lambda a, g: jnp.where(hit, a, g), arrived, got)
        values = got
    return values


def tree_reduce(values, axis, wire, first=0):
    n = lax.axis_size(axis)
    for step, fan in tree_plan(n)[first:]:
        span = step * fan
        total = values
        for j in range(1, fan):
            route = [(i + j * step, i) for i in range(0, n, span) if i + j * step < n]
            sent = jax.tree.map(lambda a: a.astype(wire), values)
            arrived = lax.ppermute(sent, axis, route)
            total = jax.tree.map(lambda t, a: t + a.astype(t.dtype), total, arrived)
        values = total
    return values


def stack_offsets(padded, before, count):
    blocks = [padded[before - offset : before - offset + count] for offset in range(before + 1)]
    return jnp.concatenate(blocks, axis=1)


def fold_offsets(grads, before, count, slots):
    result = jnp.zeros((before + count, slots) + grads.shape[2:], jnp.float32)
    for offset in range(before + 1):
        piece = grads[:, offset * slots : (offset + 1) * slots]
        result = result + jnp.pad(piece, ((before - offset, offset), (0, 0), (0, 0)))
    return result


def attend_split(q, g, k_win, v_win, k_anc, v_anc, seen_win, seen_anc, row_live):
    factor = HD ** (-0.5)
    wide = jnp.float32
    s_win = jnp.einsum("hfqd,hfkd->hfqk", q, k_win, preferred_element_type=wide) * factor
    s_anc = jnp.einsum("hfqd,hkd->hfqk", q, k_anc, preferred_element_type=wide) * factor
    s_win = jnp.where(seen_win[:, :, None, :], s_win, NEG)
    s_anc = jnp.where(seen_anc[:, :, None, :], s_anc, NEG)
    row_max = jnp.maximum(
        jnp.max(s_win, axis=3, keepdims=True), jnp.max(s_anc, axis=3, keepdims=True)
    )
    row_sum = jnp.sum(jnp.exp(s_win - row_max), axis=3, keepdims=True) + jnp.sum(
        jnp.exp(s_anc - row_max), axis=3, keepdims=True
    )
    lse = row_max + jnp.log(row_sum)
    p_win = jnp.exp(s_win - lse)
    p_anc = jnp.exp(s_anc - lse)
    pb_win = p_win.astype(jnp.bfloat16)
    pb_anc = p_anc.astype(jnp.bfloat16)
    out = jnp.einsum("hfqk,hfkd->hfqd", pb_win, v_win, preferred_element_type=wide) + jnp.einsum(
        "hfqk,hkd->hfqd", pb_anc, v_anc, preferred_element_type=wide
    )
    attn = lax.optimization_barrier(
        jnp.where(row_live[None, :, :, None], out, 0.0).astype(jnp.bfloat16)
    )
    delta = jnp.sum(g.astype(wide) * attn.astype(wide), axis=3, keepdims=True)
    dp_win = jnp.einsum("hfqd,hfkd->hfqk", g, v_win, preferred_element_type=wide)
    dp_anc = jnp.einsum("hfqd,hkd->hfqk", g, v_anc, preferred_element_type=wide)
    ds_win = (p_win * (dp_win - delta) * factor).astype(jnp.bfloat16)
    ds_anc = (p_anc * (dp_anc - delta) * factor).astype(jnp.bfloat16)
    gk_anc = jnp.einsum("hfqk,hfqd->hkd", ds_anc, q, preferred_element_type=wide)
    gv_anc = jnp.einsum("hfqk,hfqd->hkd", pb_anc, g, preferred_element_type=wide)
    gq = jnp.einsum("hfqk,hfkd->hfqd", ds_win, k_win, preferred_element_type=wide) + jnp.einsum(
        "hfqk,hkd->hfqd", ds_anc, k_anc, preferred_element_type=wide
    )
    gk_win = jnp.einsum("hfqk,hfqd->hfkd", ds_win, q, preferred_element_type=wide)
    gv_win = jnp.einsum("hfqk,hfqd->hfkd", pb_win, g, preferred_element_type=wide)
    return attn, gq, gk_win, gv_win, gk_anc, gv_anc


def on_device(q_in, k_in, v_in, q_gain, k_gain, d_out, counts, windows):
    row_count, local_width = q_in.shape
    local_heads = local_width // HD
    device = lax.axis_index("seq")
    q_float = q_in.astype(jnp.float32)
    k_float = k_in.astype(jnp.float32)
    q_power, k_power = gather_sum(
        jnp.stack([jnp.sum(q_float * q_float, axis=1), jnp.sum(k_float * k_float, axis=1)]), "tp"
    )
    q_rinv = lax.rsqrt(q_power / WIDTH + EPS)[:, None]
    k_rinv = lax.rsqrt(k_power / WIDTH + EPS)[:, None]
    q_norm = (q_float * q_rinv * q_gain).astype(jnp.bfloat16)
    k_norm = (k_float * k_rinv * k_gain).astype(jnp.bfloat16)
    padded_counts = jnp.concatenate([jnp.zeros((F_DEV,), jnp.int32), counts])
    near_counts = lax.dynamic_slice_in_dim(padded_counts, device * F_DEV, 2 * F_DEV)
    slot_index = jnp.arange(CAP, dtype=jnp.int32)
    near_live = slot_index[None, :] < near_counts[:, None]
    row_live = near_live[F_DEV:]
    grad_mask = jnp.where(row_live.reshape(row_count)[:, None], d_out, jnp.zeros_like(d_out))
    odd = device % 2 == 1
    pair_first = tree_plan(lax.axis_size("seq"))[0] == (1, 2)
    anchor = jnp.stack([k_norm[:CAP], v_in[:CAP]])
    if pair_first:
        anchor = tree_bcast(anchor, "seq", first=1)
        both = shifted(jnp.concatenate([jnp.stack([k_norm, v_in]), anchor], axis=1), "seq", 1)
        halo_k, halo_v = both[:, :row_count]
        anchor_k, anchor_v = jnp.where(odd, both[:, row_count:], anchor)
    else:
        halo_k, halo_v = shifted(jnp.stack([k_norm, v_in]), "seq", 1)
        anchor_k, anchor_v = tree_bcast(anchor, "seq")
    k_near = jnp.concatenate([halo_k, k_norm], axis=0).reshape(2 * F_DEV, CAP, local_width)
    v_near = jnp.concatenate([halo_v, v_in], axis=0).reshape(2 * F_DEV, CAP, local_width)
    def to_heads(value):
        return value.reshape(value.shape[0], value.shape[1], local_heads, HD).transpose(2, 0, 1, 3)

    def from_heads(value):
        return value.transpose(1, 2, 0, 3).reshape(value.shape[1], value.shape[2], local_heads * HD)

    def rows_to_heads(value):
        return value.reshape(value.shape[0], local_heads, HD).transpose(1, 0, 2)

    frame_local = jnp.arange(F_DEV, dtype=jnp.int32)
    offsets = jnp.arange((F_DEV + 1) * CAP, dtype=jnp.int32) // CAP
    live_stack = stack_offsets(near_live[:, :, None], F_DEV, F_DEV)[:, :, 0]
    reach = device * F_DEV + frame_local[:, None] - offsets[None, :] >= 0
    within = offsets[None, None, :] <= windows[:, None, None]
    anchor_ok = device * F_DEV + frame_local[None, :] - windows[:, None] > 0
    anchor_live = slot_index < counts[0]
    seen_win = (live_stack & reach)[None] & within
    seen_anc = anchor_ok[:, :, None] & anchor_live[None, None, :]

    q_heads = to_heads(q_norm.reshape(F_DEV, CAP, local_width))
    g_heads = to_heads(grad_mask.reshape(F_DEV, CAP, local_width))
    attn_h, grad_qh, grad_kh, grad_vh, grad_ka, grad_va = attend_split(
        q_heads,
        g_heads,
        to_heads(stack_offsets(k_near, F_DEV, F_DEV)),
        to_heads(stack_offsets(v_near, F_DEV, F_DEV)),
        rows_to_heads(anchor_k),
        rows_to_heads(anchor_v),
        seen_win,
        seen_anc,
        row_live,
    )
    attn_out = from_heads(attn_h).reshape(row_count, local_width)
    grad_qn = from_heads(grad_qh).reshape(row_count, local_width)
    grad_k_near = fold_offsets(from_heads(grad_kh), F_DEV, F_DEV, CAP)
    grad_v_near = fold_offsets(from_heads(grad_vh), F_DEV, F_DEV, CAP)
    grad_k_anchor = grad_ka.transpose(1, 0, 2).reshape(CAP, local_width)
    grad_v_anchor = grad_va.transpose(1, 0, 2).reshape(CAP, local_width)
    back = jnp.stack([grad_k_near[:F_DEV], grad_v_near[:F_DEV]]).reshape(2, row_count, local_width)
    anchor_grads = jnp.stack([grad_k_anchor, grad_v_anchor])
    if pair_first:
        both = shifted(jnp.concatenate([back, anchor_grads], axis=1), "seq", -1)
        back_k, back_v = both[:, :row_count].reshape(2, F_DEV, CAP, local_width)
        anchor_grads = anchor_grads + jnp.where(odd, 0.0, both[:, row_count:])
        anchor_gk, anchor_gv = tree_reduce(anchor_grads, "seq", jnp.bfloat16, first=1)
    else:
        back_k, back_v = shifted(back, "seq", -1).reshape(2, F_DEV, CAP, local_width)
        anchor_gk, anchor_gv = tree_reduce(anchor_grads, "seq", jnp.bfloat16)
    grad_k_own = grad_k_near[F_DEV:] + back_k
    grad_v_own = grad_v_near[F_DEV:] + back_v
    first_device = device == 0
    grad_k_own = grad_k_own.at[0].add(jnp.where(first_device, anchor_gk, 0.0))
    grad_v_own = grad_v_own.at[0].add(jnp.where(first_device, anchor_gv, 0.0))
    q_scaled = grad_qn * q_gain
    k_scaled = grad_k_own.reshape(row_count, local_width) * k_gain
    q_dot, k_dot = gather_sum(
        jnp.stack([jnp.sum(q_float * q_scaled, axis=1), jnp.sum(k_float * k_scaled, axis=1)]), "tp"
    )
    grad_q = (q_rinv * q_scaled - q_float * q_rinv**3 * q_dot[:, None] / WIDTH).astype(jnp.bfloat16)
    grad_k = (k_rinv * k_scaled - k_float * k_rinv**3 * k_dot[:, None] / WIDTH).astype(jnp.bfloat16)
    grad_v = grad_v_own.reshape(row_count, local_width).astype(jnp.bfloat16)
    return (attn_out, grad_q, grad_k, grad_v)


def solution(mesh):
    return jax.shard_map(
        on_device,
        mesh=mesh,
        in_specs=(
            P("seq", "tp"),
            P("seq", "tp"),
            P("seq", "tp"),
            P("tp"),
            P("tp"),
            P("seq", "tp"),
            P(),
            P("tp"),
        ),
        out_specs=(P("seq", "tp"), P("seq", "tp"), P("seq", "tp"), P("seq", "tp")),
        check_vma=False,
    )
```

```python
import jax
import jax.numpy as jnp
from jax import lax
from jax.sharding import PartitionSpec as P

HD = 128
CAP = 256
F_DEV = 2
WIDTH = 4096


EPS = 1e-06
NEG = -1e30


def shifted(block, axis, distance):
    devices = range(lax.axis_size(axis))
    route = [(i - distance, i) for i in devices if i - distance in devices]
    return lax.ppermute(block, axis, route)


def gather_sum(values, axis):
    n = lax.axis_size(axis)
    copies = jnp.broadcast_to(values[None], (n,) + values.shape)
    return jnp.sum(lax.all_to_all(copies, axis, 0, 0, tiled=False), axis=0)


def tree_plan(n):
    fans, m = [], n
    if m % 2 == 0 and (m.bit_length() - 1) % 2 == 1 and m & (m - 1) == 0:
        fans.append(2)
        m //= 2
    while m > 1:
        f = 4 if m % 4 == 0 else next(p for p in range(2, m + 1) if m % p == 0)
        fans.append(f)
        m //= f
    plan, step = [], 1
    for f in fans:
        plan.append((step, f))
        step *= f
    return plan


def tree_bcast(values, axis, first=0):
    n = lax.axis_size(axis)
    me = lax.axis_index(axis)
    for step, fan in reversed(tree_plan(n)[first:]):
        span = step * fan
        got = values
        for j in range(1, fan):
            route = [(i, i + j * step) for i in range(0, n, span) if i + j * step < n]
            arrived = lax.ppermute(values, axis, route)
            hit = me % span == j * step
            got = jax.tree.map(lambda a, g: jnp.where(hit, a, g), arrived, got)
        values = got
    return values


def tree_reduce(values, axis, wire, first=0):
    n = lax.axis_size(axis)
    for step, fan in tree_plan(n)[first:]:
        span = step * fan
        total = values
        for j in range(1, fan):
            route = [(i + j * step, i) for i in range(0, n, span) if i + j * step < n]
            sent = jax.tree.map(lambda a: a.astype(wire), values)
            arrived = lax.ppermute(sent, axis, route)
            total = jax.tree.map(lambda t, a: t + a.astype(t.dtype), total, arrived)
        values = total
    return values


def stack_offsets(padded, before, count):
    blocks = [padded[before - offset : before - offset + count] for offset in range(before + 1)]
    return jnp.concatenate(blocks, axis=1)


def fold_offsets(grads, before, count, slots):
    result = jnp.zeros((before + count, slots) + grads.shape[2:], jnp.float32)
    for offset in range(before + 1):
        piece = grads[:, offset * slots : (offset + 1) * slots]
        result = result + jnp.pad(piece, ((before - offset, offset), (0, 0), (0, 0)))
    return result


def attend_split(q, g, k_win, v_win, k_anc, v_anc, seen_win, seen_anc, row_live):
    factor = HD ** (-0.5)
    wide = jnp.float32
    s_win = jnp.einsum("hfqd,hfkd->hfqk", q, k_win, preferred_element_type=wide) * factor
    s_anc = jnp.einsum("hfqd,hkd->hfqk", q, k_anc, preferred_element_type=wide) * factor
    s_win = jnp.where(seen_win[:, :, None, :], s_win, NEG)
    s_anc = jnp.where(seen_anc[:, :, None, :], s_anc, NEG)
    row_max = jnp.maximum(
        jnp.max(s_win, axis=3, keepdims=True), jnp.max(s_anc, axis=3, keepdims=True)
    )
    row_sum = jnp.sum(jnp.exp(s_win - row_max), axis=3, keepdims=True) + jnp.sum(
        jnp.exp(s_anc - row_max), axis=3, keepdims=True
    )
    lse = row_max + jnp.log(row_sum)
    p_win = jnp.exp(s_win - lse)
    p_anc = jnp.exp(s_anc - lse)
    pb_win = p_win.astype(jnp.bfloat16)
    pb_anc = p_anc.astype(jnp.bfloat16)
    out = jnp.einsum("hfqk,hfkd->hfqd", pb_win, v_win, preferred_element_type=wide) + jnp.einsum(
        "hfqk,hkd->hfqd", pb_anc, v_anc, preferred_element_type=wide
    )
    attn = lax.optimization_barrier(
        jnp.where(row_live[None, :, :, None], out, 0.0).astype(jnp.bfloat16)
    )
    delta = jnp.sum(g.astype(wide) * attn.astype(wide), axis=3, keepdims=True)
    dp_win = jnp.einsum("hfqd,hfkd->hfqk", g, v_win, preferred_element_type=wide)
    dp_anc = jnp.einsum("hfqd,hkd->hfqk", g, v_anc, preferred_element_type=wide)
    ds_win = (p_win * (dp_win - delta) * factor).astype(jnp.bfloat16)
    ds_anc = (p_anc * (dp_anc - delta) * factor).astype(jnp.bfloat16)
    gk_anc = jnp.einsum("hfqk,hfqd->hkd", ds_anc, q, preferred_element_type=wide)
    gv_anc = jnp.einsum("hfqk,hfqd->hkd", pb_anc, g, preferred_element_type=wide)
    gq = jnp.einsum("hfqk,hfkd->hfqd", ds_win, k_win, preferred_element_type=wide) + jnp.einsum(
        "hfqk,hkd->hfqd", ds_anc, k_anc, preferred_element_type=wide
    )
    gk_win = jnp.einsum("hfqk,hfqd->hfkd", ds_win, q, preferred_element_type=wide)
    gv_win = jnp.einsum("hfqk,hfqd->hfkd", pb_win, g, preferred_element_type=wide)
    return attn, gq, gk_win, gv_win, gk_anc, gv_anc


def on_device(q_in, k_in, v_in, q_gain, k_gain, d_out, counts, windows):
    row_count, local_width = q_in.shape
    local_heads = local_width // HD
    device = lax.axis_index("seq")
    q_float = q_in.astype(jnp.float32)
    k_float = k_in.astype(jnp.float32)
    q_power, k_power = gather_sum(
        jnp.stack([jnp.sum(q_float * q_float, axis=1), jnp.sum(k_float * k_float, axis=1)]), "tp"
    )
    q_rinv = lax.rsqrt(q_power / WIDTH + EPS)[:, None]
    k_rinv = lax.rsqrt(k_power / WIDTH + EPS)[:, None]
    q_norm = (q_float * q_rinv * q_gain).astype(jnp.bfloat16)
    k_norm = (k_float * k_rinv * k_gain).astype(jnp.bfloat16)
    padded_counts = jnp.concatenate([jnp.zeros((F_DEV,), jnp.int32), counts])
    near_counts = lax.dynamic_slice_in_dim(padded_counts, device * F_DEV, 2 * F_DEV)
    slot_index = jnp.arange(CAP, dtype=jnp.int32)
    near_live = slot_index[None, :] < near_counts[:, None]
    row_live = near_live[F_DEV:]
    grad_mask = jnp.where(row_live.reshape(row_count)[:, None], d_out, jnp.zeros_like(d_out))
    odd = device % 2 == 1
    pair_first = tree_plan(lax.axis_size("seq"))[0] == (1, 2)
    anchor = jnp.stack([k_norm[:CAP], v_in[:CAP]])
    if pair_first:
        anchor = tree_bcast(anchor, "seq", first=1)
        both = shifted(jnp.concatenate([jnp.stack([k_norm, v_in]), anchor], axis=1), "seq", 1)
        halo_k, halo_v = both[:, :row_count]
        anchor_k, anchor_v = jnp.where(odd, both[:, row_count:], anchor)
    else:
        halo_k, halo_v = shifted(jnp.stack([k_norm, v_in]), "seq", 1)
        anchor_k, anchor_v = tree_bcast(anchor, "seq")
    k_near = jnp.concatenate([halo_k, k_norm], axis=0).reshape(2 * F_DEV, CAP, local_width)
    v_near = jnp.concatenate([halo_v, v_in], axis=0).reshape(2 * F_DEV, CAP, local_width)
    def to_heads(value):
        return value.reshape(value.shape[0], value.shape[1], local_heads, HD).transpose(2, 0, 1, 3)

    def from_heads(value):
        return value.transpose(1, 2, 0, 3).reshape(value.shape[1], value.shape[2], local_heads * HD)

    def rows_to_heads(value):
        return value.reshape(value.shape[0], local_heads, HD).transpose(1, 0, 2)

    frame_local = jnp.arange(F_DEV, dtype=jnp.int32)
    offsets = jnp.arange((F_DEV + 1) * CAP, dtype=jnp.int32) // CAP
    live_stack = stack_offsets(near_live[:, :, None], F_DEV, F_DEV)[:, :, 0]
    reach = device * F_DEV + frame_local[:, None] - offsets[None, :] >= 0
    within = offsets[None, None, :] <= windows[:, None, None]
    anchor_ok = device * F_DEV + frame_local[None, :] - windows[:, None] > 0
    anchor_live = slot_index < counts[0]
    seen_win = (live_stack & reach)[None] & within
    seen_anc = anchor_ok[:, :, None] & anchor_live[None, None, :]

    q_heads = to_heads(q_norm.reshape(F_DEV, CAP, local_width))
    g_heads = to_heads(grad_mask.reshape(F_DEV, CAP, local_width))
    attn_h, grad_qh, grad_kh, grad_vh, grad_ka, grad_va = attend_split(
        q_heads,
        g_heads,
        to_heads(stack_offsets(k_near, F_DEV, F_DEV)),
        to_heads(stack_offsets(v_near, F_DEV, F_DEV)),
        rows_to_heads(anchor_k),
        rows_to_heads(anchor_v),
        seen_win,
        seen_anc,
        row_live,
    )
    attn_out = from_heads(attn_h).reshape(row_count, local_width)
    grad_qn = from_heads(grad_qh).reshape(row_count, local_width)
    grad_k_near = fold_offsets(from_heads(grad_kh), F_DEV, F_DEV, CAP)
    grad_v_near = fold_offsets(from_heads(grad_vh), F_DEV, F_DEV, CAP)
    grad_k_anchor = grad_ka.transpose(1, 0, 2).reshape(CAP, local_width)
    grad_v_anchor = grad_va.transpose(1, 0, 2).reshape(CAP, local_width)
    back_k, back_v = shifted(jnp.stack([grad_k_near[:F_DEV], grad_v_near[:F_DEV]]), "seq", -1)
    grad_k_own = grad_k_near[F_DEV:] + back_k
    grad_v_own = grad_v_near[F_DEV:] + back_v
    anchor_gk, anchor_gv = tree_reduce(jnp.stack([grad_k_anchor, grad_v_anchor]), "seq", jnp.bfloat16)
    first_device = device == 0
    grad_k_own = grad_k_own.at[0].add(jnp.where(first_device, anchor_gk, 0.0))
    grad_v_own = grad_v_own.at[0].add(jnp.where(first_device, anchor_gv, 0.0))
    q_scaled = grad_qn * q_gain
    k_scaled = grad_k_own.reshape(row_count, local_width) * k_gain
    q_dot, k_dot = gather_sum(
        jnp.stack([jnp.sum(q_float * q_scaled, axis=1), jnp.sum(k_float * k_scaled, axis=1)]), "tp"
    )
    grad_q = (q_rinv * q_scaled - q_float * q_rinv**3 * q_dot[:, None] / WIDTH).astype(jnp.bfloat16)
    grad_k = (k_rinv * k_scaled - k_float * k_rinv**3 * k_dot[:, None] / WIDTH).astype(jnp.bfloat16)
    grad_v = grad_v_own.reshape(row_count, local_width).astype(jnp.bfloat16)
    return (attn_out, grad_q, grad_k, grad_v)


def solution(mesh):
    return jax.shard_map(
        on_device,
        mesh=mesh,
        in_specs=(
            P("seq", "tp"),
            P("seq", "tp"),
            P("seq", "tp"),
            P("tp"),
            P("tp"),
            P("seq", "tp"),
            P(),
            P("tp"),
        ),
        out_specs=(P("seq", "tp"), P("seq", "tp"), P("seq", "tp"), P("seq", "tp")),
        check_vma=False,
    )
```

```python
import jax
import jax.numpy as jnp
from jax import lax
from jax.sharding import PartitionSpec as P

HD = 128
CAP = 256
F_DEV = 2
WIDTH = 4096


EPS = 1e-06
NEG = -1e30


def shifted(block, axis, distance):
    devices = range(lax.axis_size(axis))
    route = [(i - distance, i) for i in devices if i - distance in devices]
    return lax.ppermute(block, axis, route)


def gather_sum(values, axis):
    n = lax.axis_size(axis)
    copies = jnp.broadcast_to(values[None], (n,) + values.shape)
    return jnp.sum(lax.all_to_all(copies, axis, 0, 0, tiled=False), axis=0)


def tree_plan(n):
    fans, m = [], n
    if m % 2 == 0 and (m.bit_length() - 1) % 2 == 1 and m & (m - 1) == 0:
        fans.append(2)
        m //= 2
    while m > 1:
        f = 4 if m % 4 == 0 else next(p for p in range(2, m + 1) if m % p == 0)
        fans.append(f)
        m //= f
    plan, step = [], 1
    for f in fans:
        plan.append((step, f))
        step *= f
    return plan


def tree_bcast(values, axis, first=0):
    n = lax.axis_size(axis)
    me = lax.axis_index(axis)
    for step, fan in reversed(tree_plan(n)[first:]):
        span = step * fan
        got = values
        for j in range(1, fan):
            route = [(i, i + j * step) for i in range(0, n, span) if i + j * step < n]
            arrived = lax.ppermute(values, axis, route)
            hit = me % span == j * step
            got = jax.tree.map(lambda a, g: jnp.where(hit, a, g), arrived, got)
        values = got
    return values


def tree_reduce(values, axis, wire, first=0):
    n = lax.axis_size(axis)
    for step, fan in tree_plan(n)[first:]:
        span = step * fan
        total = values
        for j in range(1, fan):
            route = [(i + j * step, i) for i in range(0, n, span) if i + j * step < n]
            sent = jax.tree.map(lambda a: a.astype(wire), values)
            arrived = lax.ppermute(sent, axis, route)
            total = jax.tree.map(lambda t, a: t + a.astype(t.dtype), total, arrived)
        values = total
    return values


def stack_offsets(padded, before, count):
    blocks = [padded[before - offset : before - offset + count] for offset in range(before + 1)]
    return jnp.concatenate(blocks, axis=1)


def fold_offsets(grads, before, count, slots):
    result = jnp.zeros((before + count, slots) + grads.shape[2:], jnp.float32)
    for offset in range(before + 1):
        piece = grads[:, offset * slots : (offset + 1) * slots]
        result = result + jnp.pad(piece, ((before - offset, offset), (0, 0), (0, 0)))
    return result


def attend_split(q, g, k_win, v_win, k_anc, v_anc, seen_win, seen_anc, row_live):
    factor = HD ** (-0.5)
    wide = jnp.float32
    s_win = jnp.einsum("hfqd,hfkd->hfqk", q, k_win, preferred_element_type=wide) * factor
    s_anc = jnp.einsum("hfqd,hkd->hfqk", q, k_anc, preferred_element_type=wide) * factor
    s_win = jnp.where(seen_win[:, :, None, :], s_win, NEG)
    s_anc = jnp.where(seen_anc[:, :, None, :], s_anc, NEG)
    row_max = jnp.maximum(
        jnp.max(s_win, axis=3, keepdims=True), jnp.max(s_anc, axis=3, keepdims=True)
    )
    row_sum = jnp.sum(jnp.exp(s_win - row_max), axis=3, keepdims=True) + jnp.sum(
        jnp.exp(s_anc - row_max), axis=3, keepdims=True
    )
    lse = row_max + jnp.log(row_sum)
    p_win = jnp.exp(s_win - lse)
    p_anc = jnp.exp(s_anc - lse)
    pb_win = p_win.astype(jnp.bfloat16)
    pb_anc = p_anc.astype(jnp.bfloat16)
    out = jnp.einsum("hfqk,hfkd->hfqd", pb_win, v_win, preferred_element_type=wide) + jnp.einsum(
        "hfqk,hkd->hfqd", pb_anc, v_anc, preferred_element_type=wide
    )
    attn = lax.optimization_barrier(
        jnp.where(row_live[None, :, :, None], out, 0.0).astype(jnp.bfloat16)
    )
    delta = jnp.sum(g.astype(wide) * attn.astype(wide), axis=3, keepdims=True)
    dp_win = jnp.einsum("hfqd,hfkd->hfqk", g, v_win, preferred_element_type=wide)
    dp_anc = jnp.einsum("hfqd,hkd->hfqk", g, v_anc, preferred_element_type=wide)
    ds_win = (p_win * (dp_win - delta) * factor).astype(jnp.bfloat16)
    ds_anc = (p_anc * (dp_anc - delta) * factor).astype(jnp.bfloat16)
    gk_anc = jnp.einsum("hfqk,hfqd->hkd", ds_anc, q, preferred_element_type=wide)
    gv_anc = jnp.einsum("hfqk,hfqd->hkd", pb_anc, g, preferred_element_type=wide)
    gq = jnp.einsum("hfqk,hfkd->hfqd", ds_win, k_win, preferred_element_type=wide) + jnp.einsum(
        "hfqk,hkd->hfqd", ds_anc, k_anc, preferred_element_type=wide
    )
    gk_win = jnp.einsum("hfqk,hfqd->hfkd", ds_win, q, preferred_element_type=wide)
    gv_win = jnp.einsum("hfqk,hfqd->hfkd", pb_win, g, preferred_element_type=wide)
    return attn, gq, gk_win, gv_win, gk_anc, gv_anc


def on_device(q_in, k_in, v_in, q_gain, k_gain, d_out, counts, windows):
    row_count, local_width = q_in.shape
    local_heads = local_width // HD
    device = lax.axis_index("seq")
    q_float = q_in.astype(jnp.float32)
    k_float = k_in.astype(jnp.float32)
    q_power, k_power = gather_sum(
        jnp.stack([jnp.sum(q_float * q_float, axis=1), jnp.sum(k_float * k_float, axis=1)]), "tp"
    )
    q_rinv = lax.rsqrt(q_power / WIDTH + EPS)[:, None]
    k_rinv = lax.rsqrt(k_power / WIDTH + EPS)[:, None]
    q_norm = (q_float * q_rinv * q_gain).astype(jnp.bfloat16)
    k_norm = (k_float * k_rinv * k_gain).astype(jnp.bfloat16)
    padded_counts = jnp.concatenate([jnp.zeros((F_DEV,), jnp.int32), counts])
    near_counts = lax.dynamic_slice_in_dim(padded_counts, device * F_DEV, 2 * F_DEV)
    slot_index = jnp.arange(CAP, dtype=jnp.int32)
    near_live = slot_index[None, :] < near_counts[:, None]
    row_live = near_live[F_DEV:]
    grad_mask = jnp.where(row_live.reshape(row_count)[:, None], d_out, jnp.zeros_like(d_out))
    odd = device % 2 == 1
    pair_first = tree_plan(lax.axis_size("seq"))[0] == (1, 2)
    anchor = jnp.stack([k_norm[:CAP], v_in[:CAP]])
    if pair_first:
        anchor = tree_bcast(anchor, "seq", first=1)
        both = shifted(jnp.concatenate([jnp.stack([k_norm, v_in]), anchor], axis=1), "seq", 1)
        halo_k, halo_v = both[:, :row_count]
        anchor_k, anchor_v = jnp.where(odd, both[:, row_count:], anchor)
    else:
        halo_k, halo_v = shifted(jnp.stack([k_norm, v_in]), "seq", 1)
        anchor_k, anchor_v = tree_bcast(anchor, "seq")
    k_near = jnp.concatenate([halo_k, k_norm], axis=0).reshape(2 * F_DEV, CAP, local_width)
    v_near = jnp.concatenate([halo_v, v_in], axis=0).reshape(2 * F_DEV, CAP, local_width)
    def to_heads(value):
        return value.reshape(value.shape[0], value.shape[1], local_heads, HD).transpose(2, 0, 1, 3)

    def from_heads(value):
        return value.transpose(1, 2, 0, 3).reshape(value.shape[1], value.shape[2], local_heads * HD)

    def rows_to_heads(value):
        return value.reshape(value.shape[0], local_heads, HD).transpose(1, 0, 2)

    frame_local = jnp.arange(F_DEV, dtype=jnp.int32)
    offsets = jnp.arange((F_DEV + 1) * CAP, dtype=jnp.int32) // CAP
    live_stack = stack_offsets(near_live[:, :, None], F_DEV, F_DEV)[:, :, 0]
    reach = device * F_DEV + frame_local[:, None] - offsets[None, :] >= 0
    within = offsets[None, None, :] <= windows[:, None, None]
    anchor_ok = device * F_DEV + frame_local[None, :] - windows[:, None] > 0
    anchor_live = slot_index < counts[0]
    seen_win = (live_stack & reach)[None] & within
    seen_anc = anchor_ok[:, :, None] & anchor_live[None, None, :]

    q_heads = to_heads(q_norm.reshape(F_DEV, CAP, local_width))
    g_heads = to_heads(grad_mask.reshape(F_DEV, CAP, local_width))
    attn_h, grad_qh, grad_kh, grad_vh, grad_ka, grad_va = attend_split(
        q_heads,
        g_heads,
        to_heads(stack_offsets(k_near, F_DEV, F_DEV)),
        to_heads(stack_offsets(v_near, F_DEV, F_DEV)),
        rows_to_heads(anchor_k),
        rows_to_heads(anchor_v),
        seen_win,
        seen_anc,
        row_live,
    )
    attn_out = from_heads(attn_h).reshape(row_count, local_width)
    grad_qn = from_heads(grad_qh).reshape(row_count, local_width)
    grad_k_near = fold_offsets(from_heads(grad_kh), F_DEV, F_DEV, CAP)
    grad_v_near = fold_offsets(from_heads(grad_vh), F_DEV, F_DEV, CAP)
    grad_k_anchor = grad_ka.transpose(1, 0, 2).reshape(CAP, local_width)
    grad_v_anchor = grad_va.transpose(1, 0, 2).reshape(CAP, local_width)
    back = jnp.stack([grad_k_near[:F_DEV], grad_v_near[:F_DEV]]).astype(jnp.bfloat16)
    back_k, back_v = shifted(back, "seq", -1).astype(jnp.float32)
    grad_k_own = grad_k_near[F_DEV:] + back_k
    grad_v_own = grad_v_near[F_DEV:] + back_v
    anchor_gk, anchor_gv = tree_reduce(jnp.stack([grad_k_anchor, grad_v_anchor]), "seq", jnp.bfloat16)
    first_device = device == 0
    grad_k_own = grad_k_own.at[0].add(jnp.where(first_device, anchor_gk, 0.0))
    grad_v_own = grad_v_own.at[0].add(jnp.where(first_device, anchor_gv, 0.0))
    q_scaled = grad_qn * q_gain
    k_scaled = grad_k_own.reshape(row_count, local_width) * k_gain
    q_dot, k_dot = gather_sum(
        jnp.stack([jnp.sum(q_float * q_scaled, axis=1), jnp.sum(k_float * k_scaled, axis=1)]), "tp"
    )
    grad_q = (q_rinv * q_scaled - q_float * q_rinv**3 * q_dot[:, None] / WIDTH).astype(jnp.bfloat16)
    grad_k = (k_rinv * k_scaled - k_float * k_rinv**3 * k_dot[:, None] / WIDTH).astype(jnp.bfloat16)
    grad_v = grad_v_own.reshape(row_count, local_width).astype(jnp.bfloat16)
    return (attn_out, grad_q, grad_k, grad_v)


def solution(mesh):
    return jax.shard_map(
        on_device,
        mesh=mesh,
        in_specs=(
            P("seq", "tp"),
            P("seq", "tp"),
            P("seq", "tp"),
            P("tp"),
            P("tp"),
            P("seq", "tp"),
            P(),
            P("tp"),
        ),
        out_specs=(P("seq", "tp"), P("seq", "tp"), P("seq", "tp"), P("seq", "tp")),
        check_vma=False,
    )
```

```python
import jax
import jax.numpy as jnp
from jax import lax
from jax.sharding import PartitionSpec as P

HD = 128
CAP = 256
F_DEV = 2
WIDTH = 4096


EPS = 1e-06
NEG = -1e30


def shifted(block, axis, distance):
    devices = range(lax.axis_size(axis))
    route = [(i - distance, i) for i in devices if i - distance in devices]
    return lax.ppermute(block, axis, route)


def gather_sum(values, axis):
    n = lax.axis_size(axis)
    copies = jnp.broadcast_to(values[None], (n,) + values.shape)
    return jnp.sum(lax.all_to_all(copies, axis, 0, 0, tiled=False), axis=0)


def tree_plan(n):
    fans, m = [], n
    if m % 2 == 0 and (m.bit_length() - 1) % 2 == 1 and m & (m - 1) == 0:
        fans.append(2)
        m //= 2
    while m > 1:
        f = 4 if m % 4 == 0 else next(p for p in range(2, m + 1) if m % p == 0)
        fans.append(f)
        m //= f
    plan, step = [], 1
    for f in fans:
        plan.append((step, f))
        step *= f
    return plan


def tree_bcast(values, axis, first=0):
    n = lax.axis_size(axis)
    me = lax.axis_index(axis)
    for step, fan in reversed(tree_plan(n)[first:]):
        span = step * fan
        got = values
        for j in range(1, fan):
            route = [(i, i + j * step) for i in range(0, n, span) if i + j * step < n]
            arrived = lax.ppermute(values, axis, route)
            hit = me % span == j * step
            got = jax.tree.map(lambda a, g: jnp.where(hit, a, g), arrived, got)
        values = got
    return values


def tree_reduce(values, axis, wire, first=0):
    n = lax.axis_size(axis)
    for step, fan in tree_plan(n)[first:]:
        span = step * fan
        total = values
        for j in range(1, fan):
            route = [(i + j * step, i) for i in range(0, n, span) if i + j * step < n]
            sent = jax.tree.map(lambda a: a.astype(wire), values)
            arrived = lax.ppermute(sent, axis, route)
            total = jax.tree.map(lambda t, a: t + a.astype(t.dtype), total, arrived)
        values = total
    return values


def stack_offsets(padded, before, count):
    blocks = [padded[before - offset : before - offset + count] for offset in range(before + 1)]
    return jnp.concatenate(blocks, axis=1)


def fold_offsets(grads, before, count, slots):
    result = jnp.zeros((before + count, slots) + grads.shape[2:], jnp.float32)
    for offset in range(before + 1):
        piece = grads[:, offset * slots : (offset + 1) * slots]
        result = result + jnp.pad(piece, ((before - offset, offset), (0, 0), (0, 0)))
    return result


def attend_split(q, g, k_win, v_win, k_anc, v_anc, seen_win, seen_anc, row_live):
    factor = HD ** (-0.5)
    wide = jnp.float32
    s_win = jnp.einsum("hfqd,hfkd->hfqk", q, k_win, preferred_element_type=wide) * factor
    s_anc = jnp.einsum("hfqd,hkd->hfqk", q, k_anc, preferred_element_type=wide) * factor
    s_win = jnp.where(seen_win[:, :, None, :], s_win, NEG)
    s_anc = jnp.where(seen_anc[:, :, None, :], s_anc, NEG)
    row_max = jnp.maximum(
        jnp.max(s_win, axis=3, keepdims=True), jnp.max(s_anc, axis=3, keepdims=True)
    )
    row_sum = jnp.sum(jnp.exp(s_win - row_max), axis=3, keepdims=True) + jnp.sum(
        jnp.exp(s_anc - row_max), axis=3, keepdims=True
    )
    lse = row_max + jnp.log(row_sum)
    p_win = jnp.exp(s_win - lse)
    p_anc = jnp.exp(s_anc - lse)
    pb_win = p_win.astype(jnp.bfloat16)
    pb_anc = p_anc.astype(jnp.bfloat16)
    out = jnp.einsum("hfqk,hfkd->hfqd", pb_win, v_win, preferred_element_type=wide) + jnp.einsum(
        "hfqk,hkd->hfqd", pb_anc, v_anc, preferred_element_type=wide
    )
    attn = lax.optimization_barrier(
        jnp.where(row_live[None, :, :, None], out, 0.0).astype(jnp.bfloat16)
    )
    delta = jnp.sum(g.astype(wide) * attn.astype(wide), axis=3, keepdims=True)
    dp_win = jnp.einsum("hfqd,hfkd->hfqk", g, v_win, preferred_element_type=wide)
    dp_anc = jnp.einsum("hfqd,hkd->hfqk", g, v_anc, preferred_element_type=wide)
    ds_win = (p_win * (dp_win - delta) * factor).astype(jnp.bfloat16)
    ds_anc = (p_anc * (dp_anc - delta) * factor).astype(jnp.bfloat16)
    gk_anc = jnp.einsum("hfqk,hfqd->hkd", ds_anc, q, preferred_element_type=wide)
    gv_anc = jnp.einsum("hfqk,hfqd->hkd", pb_anc, g, preferred_element_type=wide)
    gq = jnp.einsum("hfqk,hfkd->hfqd", ds_win, k_win, preferred_element_type=wide) + jnp.einsum(
        "hfqk,hkd->hfqd", ds_anc, k_anc, preferred_element_type=wide
    )
    gk_win = jnp.einsum("hfqk,hfqd->hfkd", ds_win, q, preferred_element_type=wide)
    gv_win = jnp.einsum("hfqk,hfqd->hfkd", pb_win, g, preferred_element_type=wide)
    return attn, gq, gk_win, gv_win, gk_anc, gv_anc


def on_device(q_in, k_in, v_in, q_gain, k_gain, d_out, counts, windows):
    row_count, local_width = q_in.shape
    local_heads = local_width // HD
    device = lax.axis_index("seq")
    q_float = q_in.astype(jnp.float32)
    q_raw, k_raw = (x.astype(jnp.float32) for x in lax.optimization_barrier((q_in, k_in)))
    k_float = k_in.astype(jnp.float32)
    q_power, k_power = gather_sum(
        jnp.stack([jnp.sum(q_raw * q_raw, axis=1), jnp.sum(k_raw * k_raw, axis=1)]), "tp"
    )
    q_rinv = lax.rsqrt(q_power / WIDTH + EPS)[:, None]
    k_rinv = lax.rsqrt(k_power / WIDTH + EPS)[:, None]
    q_norm = (q_float * q_rinv * q_gain).astype(jnp.bfloat16)
    k_norm = (k_float * k_rinv * k_gain).astype(jnp.bfloat16)
    padded_counts = jnp.concatenate([jnp.zeros((F_DEV,), jnp.int32), counts])
    near_counts = lax.dynamic_slice_in_dim(padded_counts, device * F_DEV, 2 * F_DEV)
    slot_index = jnp.arange(CAP, dtype=jnp.int32)
    near_live = slot_index[None, :] < near_counts[:, None]
    row_live = near_live[F_DEV:]
    grad_mask = jnp.where(row_live.reshape(row_count)[:, None], d_out, jnp.zeros_like(d_out))
    odd = device % 2 == 1
    pair_first = tree_plan(lax.axis_size("seq"))[0] == (1, 2)
    anchor = jnp.stack([k_norm[:CAP], v_in[:CAP]])
    if pair_first:
        anchor = tree_bcast(anchor, "seq", first=1)
        both = shifted(jnp.concatenate([jnp.stack([k_norm, v_in]), anchor], axis=1), "seq", 1)
        halo_k, halo_v = both[:, :row_count]
        anchor_k, anchor_v = jnp.where(odd, both[:, row_count:], anchor)
    else:
        halo_k, halo_v = shifted(jnp.stack([k_norm, v_in]), "seq", 1)
        anchor_k, anchor_v = tree_bcast(anchor, "seq")
    k_near = jnp.concatenate([halo_k, k_norm], axis=0).reshape(2 * F_DEV, CAP, local_width)
    v_near = jnp.concatenate([halo_v, v_in], axis=0).reshape(2 * F_DEV, CAP, local_width)
    def to_heads(value):
        return value.reshape(value.shape[0], value.shape[1], local_heads, HD).transpose(2, 0, 1, 3)

    def from_heads(value):
        return value.transpose(1, 2, 0, 3).reshape(value.shape[1], value.shape[2], local_heads * HD)

    def rows_to_heads(value):
        return value.reshape(value.shape[0], local_heads, HD).transpose(1, 0, 2)

    frame_local = jnp.arange(F_DEV, dtype=jnp.int32)
    offsets = jnp.arange((F_DEV + 1) * CAP, dtype=jnp.int32) // CAP
    live_stack = stack_offsets(near_live[:, :, None], F_DEV, F_DEV)[:, :, 0]
    reach = device * F_DEV + frame_local[:, None] - offsets[None, :] >= 0
    within = offsets[None, None, :] <= windows[:, None, None]
    anchor_ok = device * F_DEV + frame_local[None, :] - windows[:, None] > 0
    anchor_live = slot_index < counts[0]
    seen_win = (live_stack & reach)[None] & within
    seen_anc = anchor_ok[:, :, None] & anchor_live[None, None, :]

    q_heads = to_heads(q_norm.reshape(F_DEV, CAP, local_width))
    g_heads = to_heads(grad_mask.reshape(F_DEV, CAP, local_width))
    attn_h, grad_qh, grad_kh, grad_vh, grad_ka, grad_va = attend_split(
        q_heads,
        g_heads,
        to_heads(stack_offsets(k_near, F_DEV, F_DEV)),
        to_heads(stack_offsets(v_near, F_DEV, F_DEV)),
        rows_to_heads(anchor_k),
        rows_to_heads(anchor_v),
        seen_win,
        seen_anc,
        row_live,
    )
    attn_out = from_heads(attn_h).reshape(row_count, local_width)
    grad_qn = from_heads(grad_qh).reshape(row_count, local_width)
    grad_k_near = fold_offsets(from_heads(grad_kh), F_DEV, F_DEV, CAP)
    grad_v_near = fold_offsets(from_heads(grad_vh), F_DEV, F_DEV, CAP)
    grad_k_anchor = grad_ka.transpose(1, 0, 2).reshape(CAP, local_width)
    grad_v_anchor = grad_va.transpose(1, 0, 2).reshape(CAP, local_width)
    back_k, back_v = shifted(jnp.stack([grad_k_near[:F_DEV], grad_v_near[:F_DEV]]), "seq", -1)
    grad_k_own = grad_k_near[F_DEV:] + back_k
    grad_v_own = grad_v_near[F_DEV:] + back_v
    anchor_gk, anchor_gv = tree_reduce(jnp.stack([grad_k_anchor, grad_v_anchor]), "seq", jnp.bfloat16)
    first_device = device == 0
    grad_k_own = grad_k_own.at[0].add(jnp.where(first_device, anchor_gk, 0.0))
    grad_v_own = grad_v_own.at[0].add(jnp.where(first_device, anchor_gv, 0.0))
    q_scaled = grad_qn * q_gain
    k_scaled = grad_k_own.reshape(row_count, local_width) * k_gain
    q_dot, k_dot = gather_sum(
        jnp.stack([jnp.sum(q_float * q_scaled, axis=1), jnp.sum(k_float * k_scaled, axis=1)]), "tp"
    )
    grad_q = (q_rinv * q_scaled - q_float * q_rinv**3 * q_dot[:, None] / WIDTH).astype(jnp.bfloat16)
    grad_k = (k_rinv * k_scaled - k_float * k_rinv**3 * k_dot[:, None] / WIDTH).astype(jnp.bfloat16)
    grad_v = grad_v_own.reshape(row_count, local_width).astype(jnp.bfloat16)
    return (attn_out, grad_q, grad_k, grad_v)


def solution(mesh):
    return jax.shard_map(
        on_device,
        mesh=mesh,
        in_specs=(
            P("seq", "tp"),
            P("seq", "tp"),
            P("seq", "tp"),
            P("tp"),
            P("tp"),
            P("seq", "tp"),
            P(),
            P("tp"),
        ),
        out_specs=(P("seq", "tp"), P("seq", "tp"), P("seq", "tp"), P("seq", "tp")),
        check_vma=False,
    )
```

```python
import jax
import jax.numpy as jnp
from jax import lax
from jax.sharding import PartitionSpec as P

HD = 128
CAP = 256
F_DEV = 2
WIDTH = 4096


EPS = 1e-06
NEG = -1e30


def shifted(block, axis, distance):
    devices = range(lax.axis_size(axis))
    route = [(i - distance, i) for i in devices if i - distance in devices]
    return lax.ppermute(block, axis, route)


def gather_sum(values, axis):
    n = lax.axis_size(axis)
    copies = jnp.broadcast_to(values[None], (n,) + values.shape)
    return jnp.sum(lax.all_to_all(copies, axis, 0, 0, tiled=False), axis=0)


def tree_plan(n):
    fans, m = [], n
    if m % 2 == 0 and (m.bit_length() - 1) % 2 == 1 and m & (m - 1) == 0:
        fans.append(2)
        m //= 2
    while m > 1:
        f = 4 if m % 4 == 0 else next(p for p in range(2, m + 1) if m % p == 0)
        fans.append(f)
        m //= f
    plan, step = [], 1
    for f in fans:
        plan.append((step, f))
        step *= f
    return plan


def tree_bcast(values, axis, first=0):
    n = lax.axis_size(axis)
    me = lax.axis_index(axis)
    for step, fan in reversed(tree_plan(n)[first:]):
        span = step * fan
        got = values
        for j in range(1, fan):
            route = [(i, i + j * step) for i in range(0, n, span) if i + j * step < n]
            arrived = lax.ppermute(values, axis, route)
            hit = me % span == j * step
            got = jax.tree.map(lambda a, g: jnp.where(hit, a, g), arrived, got)
        values = got
    return values


def tree_reduce(values, axis, wire, first=0):
    n = lax.axis_size(axis)
    for step, fan in tree_plan(n)[first:]:
        span = step * fan
        total = values
        for j in range(1, fan):
            route = [(i + j * step, i) for i in range(0, n, span) if i + j * step < n]
            sent = jax.tree.map(lambda a: a.astype(wire), values)
            arrived = lax.ppermute(sent, axis, route)
            total = jax.tree.map(lambda t, a: t + a.astype(t.dtype), total, arrived)
        values = total
    return values


def stack_offsets(padded, before, count):
    blocks = [padded[before - offset : before - offset + count] for offset in range(before + 1)]
    return jnp.concatenate(blocks, axis=1)


def fold_offsets(grads, before, count, slots):
    result = jnp.zeros((before + count, slots) + grads.shape[2:], jnp.float32)
    for offset in range(before + 1):
        piece = grads[:, offset * slots : (offset + 1) * slots]
        result = result + jnp.pad(piece, ((before - offset, offset), (0, 0), (0, 0)))
    return result


def attend_split(q, g, k_win, v_win, k_anc, v_anc, seen_win, seen_anc, row_live):
    factor = HD ** (-0.5)
    wide = jnp.float32
    s_win = jnp.einsum("hfqd,hfkd->hfqk", q, k_win, preferred_element_type=wide) * factor
    s_anc = jnp.einsum("hfqd,hkd->hfqk", q, k_anc, preferred_element_type=wide) * factor
    s_win = jnp.where(seen_win[:, :, None, :], s_win, NEG)
    s_anc = jnp.where(seen_anc[:, :, None, :], s_anc, NEG)
    row_max = jnp.maximum(
        jnp.max(s_win, axis=3, keepdims=True), jnp.max(s_anc, axis=3, keepdims=True)
    )
    row_sum = jnp.sum(jnp.exp(s_win - row_max), axis=3, keepdims=True) + jnp.sum(
        jnp.exp(s_anc - row_max), axis=3, keepdims=True
    )
    lse = row_max + jnp.log(row_sum)
    p_win = jnp.exp(s_win - lse)
    p_anc = jnp.exp(s_anc - lse)
    pb_win = p_win.astype(jnp.bfloat16)
    pb_anc = p_anc.astype(jnp.bfloat16)
    out = jnp.einsum("hfqk,hfkd->hfqd", pb_win, v_win, preferred_element_type=wide) + jnp.einsum(
        "hfqk,hkd->hfqd", pb_anc, v_anc, preferred_element_type=wide
    )
    attn = lax.optimization_barrier(
        jnp.where(row_live[None, :, :, None], out, 0.0).astype(jnp.bfloat16)
    )
    delta = jnp.sum(g.astype(wide) * attn.astype(wide), axis=3, keepdims=True)
    dp_win = jnp.einsum("hfqd,hfkd->hfqk", g, v_win, preferred_element_type=wide)
    dp_anc = jnp.einsum("hfqd,hkd->hfqk", g, v_anc, preferred_element_type=wide)
    ds_win = (p_win * (dp_win - delta) * factor).astype(jnp.bfloat16)
    ds_anc = (p_anc * (dp_anc - delta) * factor).astype(jnp.bfloat16)
    gk_anc = jnp.einsum("hfqk,hfqd->hkd", ds_anc, q, preferred_element_type=wide)
    gv_anc = jnp.einsum("hfqk,hfqd->hkd", pb_anc, g, preferred_element_type=wide)
    gq = jnp.einsum("hfqk,hfkd->hfqd", ds_win, k_win, preferred_element_type=wide) + jnp.einsum(
        "hfqk,hkd->hfqd", ds_anc, k_anc, preferred_element_type=wide
    )
    gk_win = jnp.einsum("hfqk,hfqd->hfkd", ds_win, q, preferred_element_type=wide)
    gv_win = jnp.einsum("hfqk,hfqd->hfkd", pb_win, g, preferred_element_type=wide)
    return attn, gq, gk_win, gv_win, gk_anc, gv_anc


def on_device(q_in, k_in, v_in, q_gain, k_gain, d_out, counts, windows):
    row_count, local_width = q_in.shape
    local_heads = local_width // HD
    device = lax.axis_index("seq")
    q_float = q_in.astype(jnp.float32)
    q_raw, k_raw = (x.astype(jnp.float32) for x in lax.optimization_barrier((q_in, k_in)))
    k_float = k_in.astype(jnp.float32)
    q_power, k_power = gather_sum(
        jnp.stack([jnp.sum(q_raw * q_raw, axis=1), jnp.sum(k_raw * k_raw, axis=1)]), "tp"
    )
    q_rinv = lax.rsqrt(q_power / WIDTH + EPS)[:, None]
    k_rinv = lax.rsqrt(k_power / WIDTH + EPS)[:, None]
    q_norm = (q_float * q_rinv * q_gain).astype(jnp.bfloat16)
    k_norm = (k_float * k_rinv * k_gain).astype(jnp.bfloat16)
    padded_counts = jnp.concatenate([jnp.zeros((F_DEV,), jnp.int32), counts])
    near_counts = lax.dynamic_slice_in_dim(padded_counts, device * F_DEV, 2 * F_DEV)
    slot_index = jnp.arange(CAP, dtype=jnp.int32)
    near_live = slot_index[None, :] < near_counts[:, None]
    row_live = near_live[F_DEV:]
    grad_mask = jnp.where(row_live.reshape(row_count)[:, None], d_out, jnp.zeros_like(d_out))
    odd = device % 2 == 1
    pair_first = tree_plan(lax.axis_size("seq"))[0] == (1, 2)
    anchor = jnp.stack([k_norm[:CAP], v_in[:CAP]])
    if pair_first:
        anchor = tree_bcast(anchor, "seq", first=1)
        both = shifted(jnp.concatenate([jnp.stack([k_norm, v_in]), anchor], axis=1), "seq", 1)
        halo_k, halo_v = both[:, :row_count]
        anchor_k, anchor_v = jnp.where(odd, both[:, row_count:], anchor)
    else:
        halo_k, halo_v = shifted(jnp.stack([k_norm, v_in]), "seq", 1)
        anchor_k, anchor_v = tree_bcast(anchor, "seq")
    k_near = jnp.concatenate([halo_k, k_norm], axis=0).reshape(2 * F_DEV, CAP, local_width)
    v_near = jnp.concatenate([halo_v, v_in], axis=0).reshape(2 * F_DEV, CAP, local_width)
    def to_heads(value):
        return value.reshape(value.shape[0], value.shape[1], local_heads, HD).transpose(2, 0, 1, 3)

    def from_heads(value):
        return value.transpose(1, 2, 0, 3).reshape(value.shape[1], value.shape[2], local_heads * HD)

    def rows_to_heads(value):
        return value.reshape(value.shape[0], local_heads, HD).transpose(1, 0, 2)

    frame_local = jnp.arange(F_DEV, dtype=jnp.int32)
    offsets = jnp.arange((F_DEV + 1) * CAP, dtype=jnp.int32) // CAP
    live_stack = stack_offsets(near_live[:, :, None], F_DEV, F_DEV)[:, :, 0]
    reach = device * F_DEV + frame_local[:, None] - offsets[None, :] >= 0
    within = offsets[None, None, :] <= windows[:, None, None]
    anchor_ok = device * F_DEV + frame_local[None, :] - windows[:, None] > 0
    anchor_live = slot_index < counts[0]
    seen_win = (live_stack & reach)[None] & within
    seen_anc = anchor_ok[:, :, None] & anchor_live[None, None, :]

    q_heads = to_heads(q_norm.reshape(F_DEV, CAP, local_width))
    g_heads = to_heads(grad_mask.reshape(F_DEV, CAP, local_width))
    attn_h, grad_qh, grad_kh, grad_vh, grad_ka, grad_va = attend_split(
        q_heads,
        g_heads,
        to_heads(stack_offsets(k_near, F_DEV, F_DEV)),
        to_heads(stack_offsets(v_near, F_DEV, F_DEV)),
        rows_to_heads(anchor_k),
        rows_to_heads(anchor_v),
        seen_win,
        seen_anc,
        row_live,
    )
    attn_out = from_heads(attn_h).reshape(row_count, local_width)
    grad_qn = from_heads(grad_qh).reshape(row_count, local_width)
    grad_k_near = fold_offsets(from_heads(grad_kh), F_DEV, F_DEV, CAP)
    grad_v_near = fold_offsets(from_heads(grad_vh), F_DEV, F_DEV, CAP)
    grad_k_anchor = grad_ka.transpose(1, 0, 2).reshape(CAP, local_width)
    grad_v_anchor = grad_va.transpose(1, 0, 2).reshape(CAP, local_width)
    back_k, back_v = shifted(jnp.stack([grad_k_near[:F_DEV], grad_v_near[:F_DEV]]), "seq", -1)
    grad_k_own = grad_k_near[F_DEV:] + back_k
    grad_v_own = grad_v_near[F_DEV:] + back_v
    anchor_gk, anchor_gv = tree_reduce(jnp.stack([grad_k_anchor, grad_v_anchor]), "seq", jnp.bfloat16)
    first_device = device == 0
    grad_k_own = grad_k_own.at[0].add(jnp.where(first_device, anchor_gk, 0.0))
    grad_v_own = grad_v_own.at[0].add(jnp.where(first_device, anchor_gv, 0.0))
    q_scaled = grad_qn * q_gain
    k_scaled = grad_k_own.reshape(row_count, local_width) * k_gain
    q_dot = gather_sum(jnp.sum(q_float * q_scaled, axis=1)[None], "tp")[0]
    k_dot = gather_sum(jnp.sum(k_float * k_scaled, axis=1)[None], "tp")[0]
    grad_q = (q_rinv * q_scaled - q_float * q_rinv**3 * q_dot[:, None] / WIDTH).astype(jnp.bfloat16)
    grad_k = (k_rinv * k_scaled - k_float * k_rinv**3 * k_dot[:, None] / WIDTH).astype(jnp.bfloat16)
    grad_v = grad_v_own.reshape(row_count, local_width).astype(jnp.bfloat16)
    return (attn_out, grad_q, grad_k, grad_v)


def solution(mesh):
    return jax.shard_map(
        on_device,
        mesh=mesh,
        in_specs=(
            P("seq", "tp"),
            P("seq", "tp"),
            P("seq", "tp"),
            P("tp"),
            P("tp"),
            P("seq", "tp"),
            P(),
            P("tp"),
        ),
        out_specs=(P("seq", "tp"), P("seq", "tp"), P("seq", "tp"), P("seq", "tp")),
        check_vma=False,
    )
```

```python
import jax
import jax.numpy as jnp
from jax import lax
from jax.sharding import PartitionSpec as P

HD = 128
CAP = 256
F_DEV = 2
WIDTH = 4096


EPS = 1e-06
NEG = -1e30


def shifted(block, axis, distance):
    devices = range(lax.axis_size(axis))
    route = [(i - distance, i) for i in devices if i - distance in devices]
    return lax.ppermute(block, axis, route)


def gather_sum(values, axis):
    n = lax.axis_size(axis)
    copies = jnp.broadcast_to(values[None], (n,) + values.shape)
    return jnp.sum(lax.all_to_all(copies, axis, 0, 0, tiled=False), axis=0)


def tree_plan(n):
    fans, m = [], n
    if m % 2 == 0 and (m.bit_length() - 1) % 2 == 1 and m & (m - 1) == 0:
        fans.append(2)
        m //= 2
    while m > 1:
        f = 4 if m % 4 == 0 else next(p for p in range(2, m + 1) if m % p == 0)
        fans.append(f)
        m //= f
    plan, step = [], 1
    for f in fans:
        plan.append((step, f))
        step *= f
    return plan


def tree_bcast(values, axis, first=0):
    n = lax.axis_size(axis)
    me = lax.axis_index(axis)
    for step, fan in reversed(tree_plan(n)[first:]):
        span = step * fan
        got = values
        for j in range(1, fan):
            route = [(i, i + j * step) for i in range(0, n, span) if i + j * step < n]
            arrived = lax.ppermute(values, axis, route)
            hit = me % span == j * step
            got = jax.tree.map(lambda a, g: jnp.where(hit, a, g), arrived, got)
        values = got
    return values


def tree_reduce(values, axis, wire, first=0, last=None):
    n = lax.axis_size(axis)
    for step, fan in tree_plan(n)[first:last]:
        span = step * fan
        total = values
        for j in range(1, fan):
            route = [(i + j * step, i) for i in range(0, n, span) if i + j * step < n]
            sent = jax.tree.map(lambda a: a.astype(wire), values)
            arrived = lax.ppermute(sent, axis, route)
            total = jax.tree.map(lambda t, a: t + a.astype(t.dtype), total, arrived)
        values = total
    return values


def stack_offsets(padded, before, count):
    blocks = [padded[before - offset : before - offset + count] for offset in range(before + 1)]
    return jnp.concatenate(blocks, axis=1)


def fold_offsets(grads, before, count, slots):
    result = jnp.zeros((before + count, slots) + grads.shape[2:], jnp.float32)
    for offset in range(before + 1):
        piece = grads[:, offset * slots : (offset + 1) * slots]
        result = result + jnp.pad(piece, ((before - offset, offset), (0, 0), (0, 0)))
    return result


def attend_split(q, g, k_win, v_win, k_anc, v_anc, seen_win, seen_anc, row_live):
    factor = HD ** (-0.5)
    wide = jnp.float32
    s_win = jnp.einsum("hfqd,hfkd->hfqk", q, k_win, preferred_element_type=wide) * factor
    s_anc = jnp.einsum("hfqd,hkd->hfqk", q, k_anc, preferred_element_type=wide) * factor
    s_win = jnp.where(seen_win[:, :, None, :], s_win, NEG)
    s_anc = jnp.where(seen_anc[:, :, None, :], s_anc, NEG)
    row_max = jnp.maximum(
        jnp.max(s_win, axis=3, keepdims=True), jnp.max(s_anc, axis=3, keepdims=True)
    )
    row_sum = jnp.sum(jnp.exp(s_win - row_max), axis=3, keepdims=True) + jnp.sum(
        jnp.exp(s_anc - row_max), axis=3, keepdims=True
    )
    lse = row_max + jnp.log(row_sum)
    p_win = jnp.exp(s_win - lse)
    p_anc = jnp.exp(s_anc - lse)
    pb_win = p_win.astype(jnp.bfloat16)
    pb_anc = p_anc.astype(jnp.bfloat16)
    out = jnp.einsum("hfqk,hfkd->hfqd", pb_win, v_win, preferred_element_type=wide) + jnp.einsum(
        "hfqk,hkd->hfqd", pb_anc, v_anc, preferred_element_type=wide
    )
    attn = lax.optimization_barrier(
        jnp.where(row_live[None, :, :, None], out, 0.0).astype(jnp.bfloat16)
    )
    delta = jnp.sum(g.astype(wide) * attn.astype(wide), axis=3, keepdims=True)
    dp_win = jnp.einsum("hfqd,hfkd->hfqk", g, v_win, preferred_element_type=wide)
    dp_anc = jnp.einsum("hfqd,hkd->hfqk", g, v_anc, preferred_element_type=wide)
    ds_win = (p_win * (dp_win - delta) * factor).astype(jnp.bfloat16)
    ds_anc = (p_anc * (dp_anc - delta) * factor).astype(jnp.bfloat16)
    gk_anc = jnp.einsum("hfqk,hfqd->hkd", ds_anc, q, preferred_element_type=wide)
    gv_anc = jnp.einsum("hfqk,hfqd->hkd", pb_anc, g, preferred_element_type=wide)
    gq = jnp.einsum("hfqk,hfkd->hfqd", ds_win, k_win, preferred_element_type=wide) + jnp.einsum(
        "hfqk,hkd->hfqd", ds_anc, k_anc, preferred_element_type=wide
    )
    gk_win = jnp.einsum("hfqk,hfqd->hfkd", ds_win, q, preferred_element_type=wide)
    gv_win = jnp.einsum("hfqk,hfqd->hfkd", pb_win, g, preferred_element_type=wide)
    return attn, gq, gk_win, gv_win, gk_anc, gv_anc


def on_device(q_in, k_in, v_in, q_gain, k_gain, d_out, counts, windows):
    row_count, local_width = q_in.shape
    local_heads = local_width // HD
    device = lax.axis_index("seq")
    q_float = q_in.astype(jnp.float32)
    q_raw, k_raw = (x.astype(jnp.float32) for x in lax.optimization_barrier((q_in, k_in)))
    k_float = k_in.astype(jnp.float32)
    q_power, k_power = gather_sum(
        jnp.stack([jnp.sum(q_raw * q_raw, axis=1), jnp.sum(k_raw * k_raw, axis=1)]), "tp"
    )
    q_rinv = lax.rsqrt(q_power / WIDTH + EPS)[:, None]
    k_rinv = lax.rsqrt(k_power / WIDTH + EPS)[:, None]
    q_norm = (q_float * q_rinv * q_gain).astype(jnp.bfloat16)
    k_norm = (k_float * k_rinv * k_gain).astype(jnp.bfloat16)
    padded_counts = jnp.concatenate([jnp.zeros((F_DEV,), jnp.int32), counts])
    near_counts = lax.dynamic_slice_in_dim(padded_counts, device * F_DEV, 2 * F_DEV)
    slot_index = jnp.arange(CAP, dtype=jnp.int32)
    near_live = slot_index[None, :] < near_counts[:, None]
    row_live = near_live[F_DEV:]
    grad_mask = jnp.where(row_live.reshape(row_count)[:, None], d_out, jnp.zeros_like(d_out))
    odd = device % 2 == 1
    pair_first = tree_plan(lax.axis_size("seq"))[0] == (1, 2)
    anchor = jnp.stack([k_norm[:CAP], v_in[:CAP]])
    if pair_first:
        anchor = tree_bcast(anchor, "seq", first=1)
        both = shifted(jnp.concatenate([jnp.stack([k_norm, v_in]), anchor], axis=1), "seq", 1)
        halo_k, halo_v = both[:, :row_count]
        anchor_k, anchor_v = jnp.where(odd, both[:, row_count:], anchor)
    else:
        halo_k, halo_v = shifted(jnp.stack([k_norm, v_in]), "seq", 1)
        anchor_k, anchor_v = tree_bcast(anchor, "seq")
    k_near = jnp.concatenate([halo_k, k_norm], axis=0).reshape(2 * F_DEV, CAP, local_width)
    v_near = jnp.concatenate([halo_v, v_in], axis=0).reshape(2 * F_DEV, CAP, local_width)
    def to_heads(value):
        return value.reshape(value.shape[0], value.shape[1], local_heads, HD).transpose(2, 0, 1, 3)

    def from_heads(value):
        return value.transpose(1, 2, 0, 3).reshape(value.shape[1], value.shape[2], local_heads * HD)

    def rows_to_heads(value):
        return value.reshape(value.shape[0], local_heads, HD).transpose(1, 0, 2)

    frame_local = jnp.arange(F_DEV, dtype=jnp.int32)
    offsets = jnp.arange((F_DEV + 1) * CAP, dtype=jnp.int32) // CAP
    live_stack = stack_offsets(near_live[:, :, None], F_DEV, F_DEV)[:, :, 0]
    reach = device * F_DEV + frame_local[:, None] - offsets[None, :] >= 0
    within = offsets[None, None, :] <= windows[:, None, None]
    anchor_ok = device * F_DEV + frame_local[None, :] - windows[:, None] > 0
    anchor_live = slot_index < counts[0]
    seen_win = (live_stack & reach)[None] & within
    seen_anc = anchor_ok[:, :, None] & anchor_live[None, None, :]

    q_heads = to_heads(q_norm.reshape(F_DEV, CAP, local_width))
    g_heads = to_heads(grad_mask.reshape(F_DEV, CAP, local_width))
    attn_h, grad_qh, grad_kh, grad_vh, grad_ka, grad_va = attend_split(
        q_heads,
        g_heads,
        to_heads(stack_offsets(k_near, F_DEV, F_DEV)),
        to_heads(stack_offsets(v_near, F_DEV, F_DEV)),
        rows_to_heads(anchor_k),
        rows_to_heads(anchor_v),
        seen_win,
        seen_anc,
        row_live,
    )
    attn_out = from_heads(attn_h).reshape(row_count, local_width)
    grad_qn = from_heads(grad_qh).reshape(row_count, local_width)
    grad_k_near = fold_offsets(from_heads(grad_kh), F_DEV, F_DEV, CAP)
    grad_v_near = fold_offsets(from_heads(grad_vh), F_DEV, F_DEV, CAP)
    grad_k_anchor = grad_ka.transpose(1, 0, 2).reshape(CAP, local_width)
    grad_v_anchor = grad_va.transpose(1, 0, 2).reshape(CAP, local_width)
    anchor_grads = tree_reduce(
        jnp.stack([grad_k_anchor, grad_v_anchor]), "seq", jnp.bfloat16, last=2
    )
    back, anchor_grads = lax.optimization_barrier(
        (jnp.stack([grad_k_near[:F_DEV], grad_v_near[:F_DEV]]), anchor_grads)
    )
    anchor_gk, anchor_gv = tree_reduce(anchor_grads, "seq", jnp.bfloat16, first=2)
    back_k, back_v = shifted(back, "seq", -1)
    grad_k_own = grad_k_near[F_DEV:] + back_k
    grad_v_own = grad_v_near[F_DEV:] + back_v
    first_device = device == 0
    grad_k_own = grad_k_own.at[0].add(jnp.where(first_device, anchor_gk, 0.0))
    grad_v_own = grad_v_own.at[0].add(jnp.where(first_device, anchor_gv, 0.0))
    q_scaled = grad_qn * q_gain
    k_scaled = grad_k_own.reshape(row_count, local_width) * k_gain
    q_dot, k_dot = gather_sum(
        jnp.stack([jnp.sum(q_float * q_scaled, axis=1), jnp.sum(k_float * k_scaled, axis=1)]), "tp"
    )
    grad_q = (q_rinv * q_scaled - q_float * q_rinv**3 * q_dot[:, None] / WIDTH).astype(jnp.bfloat16)
    grad_k = (k_rinv * k_scaled - k_float * k_rinv**3 * k_dot[:, None] / WIDTH).astype(jnp.bfloat16)
    grad_v = grad_v_own.reshape(row_count, local_width).astype(jnp.bfloat16)
    return (attn_out, grad_q, grad_k, grad_v)


def solution(mesh):
    return jax.shard_map(
        on_device,
        mesh=mesh,
        in_specs=(
            P("seq", "tp"),
            P("seq", "tp"),
            P("seq", "tp"),
            P("tp"),
            P("tp"),
            P("seq", "tp"),
            P(),
            P("tp"),
        ),
        out_specs=(P("seq", "tp"), P("seq", "tp"), P("seq", "tp"), P("seq", "tp")),
        check_vma=False,
    )
```
